128 devices in a mesh: wl: 8 (over x, z_hi), tile: 16 (over z_lo, y, core).
Axes of the slice: x: 4, y: 4, z: 4 (z_hi: 2, z_lo: 2; z = z_hi * 2 + z_lo), core: 2. Of those that a mesh axis runs over, the one named last changes fastest.
Arguments:
- density: float32 [32, 1024], P('tile', 'wl'), may hold values from 0 to 1
- foot_index: int32 [4, 128, 4096], P(None, 'tile'), may hold values from 0 to 2047, as said below
- foot_weight: bfloat16 [4, 128, 4096], P(None, 'tile'), may hold values from 0.099609375 to 0.3984375
- source_fwd: float32 [16, 128, 4096], P('wl', 'tile'), may hold values from -6 to 6
- source_adj: float32 [16, 128, 4096], P('wl', 'tile'), may hold values from -6 to 6
- omega: float32 [16], P('wl'), may hold values from 0.2 to 1.5
Outputs:
- forward_field: float32 [16, 128, 4096], P('wl', 'tile')
- density_grad: float32 [32, 1024], P('tile', 'wl')
The draws below stay inside these ranges and needn't reach their ends.
Inputs may be any that keep to these rules, and one draw needn't show every extreme that they name: foot_index[f, x, y] = r * 1024 + c names coarse row r and column c of the strip of the tile holding row x, with r within one of (x mod 8) // 4 and c within two of y // 4; entry f = 0 is the cell's own block.
All inputs are finite; a program needn't handle non-finite values.
Results may differ from the reference program's by a relative error of at most 0.0003.
Values sent between devices are 32-bit elements; how exact they have to be, the bound alone decides.
No kernel may reach another device: no remote copies, remote signals or barrier semaphores. Data moves between devices by JAX's collectives and lax.ppermute only.
A program may use at most 192 MiB of HBM per device.

```python
import math
import jax
import jax.numpy as jnp
from jax import lax

CX = 8
NY = 4096
FOOT = 4
ITERS = 4
NX = 128
BX = 32
BY = 1024
WL = 16


def draw_foot_index(key, part):
    key_row, key_col = jax.random.split(jax.random.fold_in(key, 11))
    row_shift = jax.random.randint(key_row, (FOOT, NX, NY), -1, 2)
    col_shift = jax.random.randint(key_col, (FOOT, NX, NY), -2, 3)
    entry = jnp.arange(FOOT, dtype=jnp.int32)[:, None, None]
    keep = (entry > 0).astype(jnp.int32)
    row_shift = row_shift * keep
    col_shift = col_shift * keep
    rows = jnp.arange(NX, dtype=jnp.int32)[None, :, None]
    cols = jnp.arange(NY, dtype=jnp.int32)[None, None, :]
    block_row = jnp.clip(rows % CX // 4 + row_shift, 0, CX // 4 - 1)
    block_col = jnp.clip(cols // 4 + col_shift, 0, NY // 4 - 1)
    return (block_row * (NY // 4) + block_col).astype(jnp.int32)


def block_levels(rng, shape, pieces, least, top_value):
    def one(dim, shards_of):
        steps = jax.random.uniform(jax.random.fold_in(jax.random.fold_in(rng, 6), dim), (shards_of,), jnp.float32, least / len(pieces), top_value / len(pieces))
        return jnp.repeat(jnp.exp(steps), shape[dim] // shards_of).reshape((-1,) + (1,) * (len(shape) - dim - 1))

    level = one(*pieces[0])
    for cut in pieces[1:]:
        level = level * one(*cut)
    return level


def gaussian(own_key, shape, width, reach, cuts=(), held_as=jnp.bfloat16):
    entries = width * jax.random.normal(own_key, shape, jnp.float32)
    if cuts:
        entries = entries * block_levels(own_key, shape, cuts, -0.22, 0.18)
    return jnp.clip(entries, -reach, reach).astype(held_as)


def setup_inputs(seed: int = 0) -> dict:
    key_of = jax.random.split(jax.random.key(seed), 7)
    return {
        "density": jnp.clip(1.0 * jax.random.uniform(key_of[0], (BX, BY), jnp.float32) ** block_levels(key_of[0], (BX, BY), ((0, 16), (1, 8)), -0.2, 0.2), 0.0, 1.0),
        "foot_index": draw_foot_index(jax.random.fold_in(key_of[6], 71), 0),
        "foot_weight": jnp.clip(0.099609375 + 0.29882812 * jax.random.uniform(key_of[2], (FOOT, NX, NY), jnp.float32) ** block_levels(key_of[2], (FOOT, NX, NY), ((1, 16),), -0.2, 0.2), 0.099609375, 0.3984375).astype(jnp.bfloat16),
        "source_fwd": gaussian(key_of[3], (WL, NX, NY), 1.0, 6.0, ((0, 8), (1, 16)), jnp.float32),
        "source_adj": gaussian(key_of[4], (WL, NX, NY), 1.0, 6.0, ((0, 8), (1, 16)), jnp.float32),
        "omega": jnp.clip(jnp.exp(math.log(1.5) - 2.014903 * jax.random.uniform(key_of[5], (WL,), jnp.float32) ** block_levels(key_of[5], (WL,), ((0, 8),), -0.2, 0.2)), 0.2, 1.5),
    }


time_step = 0.5
high_contrast = 4.0
drude_decay = 0.9
drude_gain = 0.5


def march(source, omega, density_cell, inverse):
    field_e = jnp.zeros_like(source)
    field_hx = jnp.zeros_like(source)
    field_hy = jnp.zeros_like(source)
    current = jnp.zeros_like(source)
    history = []
    for turn in range(ITERS):
        row_zero = jnp.zeros_like(source[:, :1, :])
        col_zero = jnp.zeros_like(source[:, :, :1])
        e_up = jnp.concatenate([field_e[:, 1:, :], row_zero], 1)
        e_right = jnp.concatenate([field_e[:, :, 1:], col_zero], 2)
        field_hx = field_hx - time_step * (e_right - field_e)
        field_hy = field_hy + time_step * (e_up - field_e)
        current = drude_decay * current + drude_gain * density_cell * field_e
        hy_down = jnp.concatenate([row_zero, field_hy[:, :-1, :]], 1)
        hx_left = jnp.concatenate([col_zero, field_hx[:, :, :-1]], 2)
        drive = jnp.sin(omega * (turn + 1.0))
        field_e = field_e + inverse * ((field_hy - hy_down) - (field_hx - hx_left) - current) + drive * source
        history.append(field_e)
    sense = jnp.zeros_like(source[0])
    for turn in range(ITERS):
        sense = sense + history[turn][1] * history[ITERS - 1 - turn][0]
    return field_e[0], sense


def reference(density, foot_index, foot_weight, source_fwd, source_adj, omega):
    rows = jnp.arange(NX, dtype=jnp.int32)
    offset = ((rows // CX) * ((CX // 4) * BY)).astype(jnp.int32)
    global_index = foot_index + offset[None, :, None]
    weights = foot_weight.astype(jnp.float32)
    flat = density.reshape(-1)
    density_cell = jnp.sum(weights * flat[global_index], axis=0)
    permittivity = 1.0 + high_contrast * density_cell
    inverse = time_step / permittivity

    def one(total, inputs):
        fwd, adj, freq = inputs
        final, sense = march(jnp.stack([fwd, adj]), freq, density_cell, inverse)
        return total + sense, final

    total, finals = lax.scan(one, jnp.zeros((NX, NY), jnp.float32), (source_fwd, source_adj, omega))
    values = (high_contrast / WL) * weights * total[None]
    grad = jax.ops.segment_sum(values.reshape(-1), global_index.reshape(-1), num_segments=BX * BY)
    return finals, grad.reshape(BX, BY)
```

```python
import jax
import jax.numpy as jnp
from jax import lax
from jax.sharding import PartitionSpec as P

ITERS = 4
HALO = 4
SHIFTS = (-2, -1, 0, 1, 2)


time_step = 0.5
high_contrast = 4.0
drude_decay = 0.9
drude_gain = 0.5


def from_behind(value, axis, steps):
    count = lax.axis_size(axis)
    first, last = (max(0, -steps), min(count, count - steps))
    return lax.ppermute(value, axis, [(source, source + steps) for source in range(first, last)])


def with_halo(value, axis):
    above = from_behind(value[..., -HALO:, :], axis, 1)
    below = from_behind(value[..., :HALO, :], axis, -1)
    return jnp.concatenate([above, value, below], axis=-2)


def lane_shift(vector, shift):
    width = vector.shape[-1]
    pad = [(0, 0)] * (vector.ndim - 1) + [(abs(shift), abs(shift))]
    padded = jnp.pad(vector, pad)
    start = abs(shift) - shift
    return lax.slice_in_dim(padded, start, start + width, axis=vector.ndim - 1)


def march(source, drive, density_cell, inverse, valid):
    field_e = jnp.zeros_like(source)
    field_hx = jnp.zeros_like(source)
    field_hy = jnp.zeros_like(source)
    current = jnp.zeros_like(source)
    rows = source.shape[2]
    history = []
    for turn in range(ITERS):
        row_zero = jnp.zeros_like(source[:, :, :1, :])
        col_zero = jnp.zeros_like(source[:, :, :, :1])
        e_up = jnp.concatenate([field_e[:, :, 1:, :], row_zero], 2)
        e_right = jnp.concatenate([field_e[:, :, :, 1:], col_zero], 3)
        field_hx = field_hx - time_step * (e_right - field_e)
        field_hy = (field_hy + time_step * (e_up - field_e)) * valid
        current = drude_decay * current + drude_gain * density_cell * field_e
        hy_down = jnp.concatenate([row_zero, field_hy[:, :, :-1, :]], 2)
        hx_left = jnp.concatenate([col_zero, field_hx[:, :, :, :-1]], 3)
        field_e = (
            field_e
            + inverse * (field_hy - hy_down - (field_hx - hx_left) - current)
            + drive[turn] * source
        ) * valid
        history.append(field_e[:, :, HALO : rows - HALO, :])
    return history


def shards(density, foot_index, foot_weight, source_fwd, source_adj, omega):
    sources = jnp.stack([source_fwd, source_adj])
    sources_ext = with_halo(sources, "tile")
    strip = lax.all_gather(density, "wl", axis=1, tiled=True)
    block_rows, block_cols = strip.shape
    cells_x, cells_y = foot_index.shape[1:]
    factor = cells_y // block_cols
    weights = foot_weight.astype(jnp.float32)
    col_block = lax.broadcasted_iota(jnp.int32, (1, cells_y), 1) // factor
    key = (foot_index // block_cols) * len(SHIFTS) + (foot_index % block_cols - col_block[None]) + 2
    upsampled = jnp.repeat(strip, factor, axis=1)
    matched = []
    density_cell = jnp.zeros((cells_x, cells_y), jnp.float32)
    for row in range(block_rows):
        for slot, shift in enumerate(SHIFTS):
            code = row * len(SHIFTS) + slot
            weight_sum = jnp.sum(jnp.where(key == code, weights, 0.0), axis=0)
            matched.append(weight_sum)
            density_cell = density_cell + weight_sum * lane_shift(upsampled[row], -factor * shift)[None]
    density_ext = with_halo(density_cell, "tile")
    inverse_ext = time_step / (1.0 + high_contrast * density_ext)
    rows_ext = cells_x + 2 * HALO
    global_row = lax.axis_index("tile") * cells_x - HALO + lax.broadcasted_iota(jnp.int32, (rows_ext, 1), 0)
    valid = ((global_row >= 0) & (global_row < cells_x * lax.axis_size("tile"))).astype(jnp.float32)
    drive = [jnp.sin(omega * (turn + 1.0))[None, :, None, None] for turn in range(ITERS)]
    history = march(sources_ext, drive, density_ext, inverse_ext, valid)
    sense = jnp.zeros((cells_x, cells_y), jnp.float32)
    for turn in range(ITERS):
        sense = sense + jnp.sum(history[turn][1] * history[ITERS - 1 - turn][0], axis=0)
    total_waves = source_fwd.shape[0] * lax.axis_size("wl")
    scaled = high_contrast / total_waves * sense
    pooled_rows = []
    for row in range(block_rows):
        acc = jnp.zeros((cells_y,), jnp.float32)
        for slot, shift in enumerate(SHIFTS):
            per_col = jnp.sum(matched[row * len(SHIFTS) + slot] * scaled, axis=0)
            acc = acc + lane_shift(per_col, factor * shift)
        pooled_rows.append(acc.reshape(block_cols, factor).sum(axis=1))
    partial_grad = jnp.stack(pooled_rows)
    density_grad = lax.psum_scatter(partial_grad, "wl", scatter_dimension=1, tiled=True)
    return (history[ITERS - 1][0], density_grad)


def solution(mesh):
    in_specs = (
        P("tile", "wl"),
        P(None, "tile", None),
        P(None, "tile", None),
        P("wl", "tile", None),
        P("wl", "tile", None),
        P("wl"),
    )
    out_specs = (P("wl", "tile", None), P("tile", "wl"))
    return jax.shard_map(shards, mesh=mesh, in_specs=in_specs, out_specs=out_specs, check_vma=False)
```

```python
import jax
import jax.numpy as jnp
from jax import lax
from jax.sharding import PartitionSpec as P

ITERS = 4
HALO = 4
SHIFTS = (-2, -1, 0, 1, 2)


time_step = 0.5
high_contrast = 4.0
drude_decay = 0.9
drude_gain = 0.5


def from_behind(value, axis, steps):
    count = lax.axis_size(axis)
    first, last = (max(0, -steps), min(count, count - steps))
    return lax.ppermute(value, axis, [(source, source + steps) for source in range(first, last)])


def with_halo(value, axis):
    above = from_behind(value[..., -HALO:, :], axis, 1)
    below = from_behind(value[..., :HALO, :], axis, -1)
    return jnp.concatenate([above, value, below], axis=-2)


def gather_columns(value, axis):
    count = lax.axis_size(axis)
    copies = jnp.broadcast_to(value[None], (count,) + value.shape)
    pieces = lax.all_to_all(copies, axis, 0, 0, tiled=True)
    return pieces.transpose(1, 0, 2).reshape(value.shape[0], count * value.shape[1])


def scatter_sum_columns(value, axis):
    count = lax.axis_size(axis)
    rows, cols = value.shape
    pieces = value.reshape(rows, count, cols // count).transpose(1, 0, 2)
    return lax.all_to_all(pieces, axis, 0, 0, tiled=True).sum(axis=0)


def lane_shift(vector, shift):
    width = vector.shape[-1]
    pad = [(0, 0)] * (vector.ndim - 1) + [(abs(shift), abs(shift))]
    padded = jnp.pad(vector, pad)
    start = abs(shift) - shift
    return lax.slice_in_dim(padded, start, start + width, axis=vector.ndim - 1)


def march(source, drive, density_cell, inverse, valid):
    field_e = jnp.zeros_like(source)
    field_hx = jnp.zeros_like(source)
    field_hy = jnp.zeros_like(source)
    current = jnp.zeros_like(source)
    rows = source.shape[2]
    history = []
    for turn in range(ITERS):
        row_zero = jnp.zeros_like(source[:, :, :1, :])
        col_zero = jnp.zeros_like(source[:, :, :, :1])
        e_up = jnp.concatenate([field_e[:, :, 1:, :], row_zero], 2)
        e_right = jnp.concatenate([field_e[:, :, :, 1:], col_zero], 3)
        field_hx = field_hx - time_step * (e_right - field_e)
        field_hy = (field_hy + time_step * (e_up - field_e)) * valid
        current = drude_decay * current + drude_gain * density_cell * field_e
        hy_down = jnp.concatenate([row_zero, field_hy[:, :, :-1, :]], 2)
        hx_left = jnp.concatenate([col_zero, field_hx[:, :, :, :-1]], 3)
        field_e = (
            field_e
            + inverse * (field_hy - hy_down - (field_hx - hx_left) - current)
            + drive[turn] * source
        ) * valid
        history.append(field_e[:, :, HALO : rows - HALO, :])
    return history


def shards(density, foot_index, foot_weight, source_fwd, source_adj, omega):
    sources = jnp.stack([source_fwd, source_adj])
    sources_ext = with_halo(sources, "tile")
    strip = gather_columns(density, "wl")
    block_rows, block_cols = strip.shape
    cells_x, cells_y = foot_index.shape[1:]
    factor = cells_y // block_cols
    weights = foot_weight.astype(jnp.float32)
    col_block = lax.broadcasted_iota(jnp.int32, (1, cells_y), 1) // factor
    key = (foot_index // block_cols) * len(SHIFTS) + (foot_index % block_cols - col_block[None]) + 2
    upsampled = jnp.repeat(strip, factor, axis=1)
    matched = []
    density_cell = jnp.zeros((cells_x, cells_y), jnp.float32)
    for row in range(block_rows):
        for slot, shift in enumerate(SHIFTS):
            code = row * len(SHIFTS) + slot
            weight_sum = jnp.sum(jnp.where(key == code, weights, 0.0), axis=0)
            matched.append(weight_sum)
            density_cell = density_cell + weight_sum * lane_shift(upsampled[row], -factor * shift)[None]
    density_ext = with_halo(density_cell, "tile")
    inverse_ext = time_step / (1.0 + high_contrast * density_ext)
    rows_ext = cells_x + 2 * HALO
    global_row = lax.axis_index("tile") * cells_x - HALO + lax.broadcasted_iota(jnp.int32, (rows_ext, 1), 0)
    valid = ((global_row >= 0) & (global_row < cells_x * lax.axis_size("tile"))).astype(jnp.float32)
    drive = [jnp.sin(omega * (turn + 1.0))[None, :, None, None] for turn in range(ITERS)]
    history = march(sources_ext, drive, density_ext, inverse_ext, valid)
    sense = jnp.zeros((cells_x, cells_y), jnp.float32)
    for turn in range(ITERS):
        sense = sense + jnp.sum(history[turn][1] * history[ITERS - 1 - turn][0], axis=0)
    total_waves = source_fwd.shape[0] * lax.axis_size("wl")
    scaled = high_contrast / total_waves * sense
    pooled_rows = []
    for row in range(block_rows):
        acc = jnp.zeros((cells_y,), jnp.float32)
        for slot, shift in enumerate(SHIFTS):
            per_col = jnp.sum(matched[row * len(SHIFTS) + slot] * scaled, axis=0)
            acc = acc + lane_shift(per_col, factor * shift)
        pooled_rows.append(acc.reshape(block_cols, factor).sum(axis=1))
    partial_grad = jnp.stack(pooled_rows)
    density_grad = scatter_sum_columns(partial_grad, "wl")
    return (history[ITERS - 1][0], density_grad)


def solution(mesh):
    in_specs = (
        P("tile", "wl"),
        P(None, "tile", None),
        P(None, "tile", None),
        P("wl", "tile", None),
        P("wl", "tile", None),
        P("wl"),
    )
    out_specs = (P("wl", "tile", None), P("tile", "wl"))
    return jax.shard_map(shards, mesh=mesh, in_specs=in_specs, out_specs=out_specs, check_vma=False)
```

```python
import jax
import jax.numpy as jnp
from jax import lax
from jax.sharding import PartitionSpec as P

ITERS = 4
HALO = 4
SHIFTS = (-2, -1, 0, 1, 2)


time_step = 0.5
high_contrast = 4.0
drude_decay = 0.9
drude_gain = 0.5


def from_behind(value, axis, steps):
    count = lax.axis_size(axis)
    first, last = (max(0, -steps), min(count, count - steps))
    return lax.ppermute(value, axis, [(source, source + steps) for source in range(first, last)])


def with_halo(value, axis):
    above = from_behind(value[..., -HALO:, :], axis, 1)
    below = from_behind(value[..., :HALO, :], axis, -1)
    return jnp.concatenate([above, value, below], axis=-2)


def gather_columns(value, axis):
    count = lax.axis_size(axis)
    copies = jnp.broadcast_to(value[None], (count,) + value.shape)
    pieces = lax.all_to_all(copies, axis, 0, 0, tiled=True)
    return pieces.transpose(1, 0, 2).reshape(value.shape[0], count * value.shape[1])


def scatter_sum_columns(value, axis):
    count = lax.axis_size(axis)
    rows, cols = value.shape
    pieces = value.reshape(rows, count, cols // count).transpose(1, 0, 2)
    return lax.all_to_all(pieces, axis, 0, 0, tiled=True).sum(axis=0)


def lane_shift(vector, shift):
    width = vector.shape[-1]
    pad = [(0, 0)] * (vector.ndim - 1) + [(abs(shift), abs(shift))]
    padded = jnp.pad(vector, pad)
    start = abs(shift) - shift
    return lax.slice_in_dim(padded, start, start + width, axis=vector.ndim - 1)


def march(source, drive, density_cell, inverse, hy_step):
    field_e = jnp.zeros_like(source)
    field_hx = jnp.zeros_like(source)
    field_hy = jnp.zeros_like(source)
    current = jnp.zeros_like(source)
    history = []
    for turn in range(ITERS):
        row_zero = jnp.zeros_like(source[:, :, :1, :])
        col_zero = jnp.zeros_like(source[:, :, :, :1])
        e_up = jnp.concatenate([field_e[:, :, 1:, :], row_zero], 2)
        e_right = jnp.concatenate([field_e[:, :, :, 1:], col_zero], 3)
        field_hx = field_hx - time_step * (e_right - field_e)
        field_hy = field_hy + hy_step * (e_up - field_e)
        current = drude_decay * current + drude_gain * density_cell * field_e
        hy_down = jnp.concatenate([row_zero, field_hy[:, :, :-1, :]], 2)
        hx_left = jnp.concatenate([col_zero, field_hx[:, :, :, :-1]], 3)
        field_e = (
            field_e
            + inverse * (field_hy - hy_down - (field_hx - hx_left) - current)
            + drive[turn] * source
        )
        history.append(field_e)
    return history


def shards(density, foot_index, foot_weight, source_fwd, source_adj, omega):
    sources = jnp.stack([source_fwd, source_adj])
    sources_ext = with_halo(sources, "tile")
    strip = gather_columns(density, "wl")
    block_rows, block_cols = strip.shape
    cells_x, cells_y = foot_index.shape[1:]
    factor = cells_y // block_cols
    weights = foot_weight.astype(jnp.float32)
    col_block = lax.broadcasted_iota(jnp.int32, (1, cells_y), 1) // factor
    key = (foot_index // block_cols) * len(SHIFTS) + (foot_index % block_cols - col_block[None]) + 2
    codes = lax.broadcasted_iota(jnp.int32, (block_rows * len(SHIFTS), 1, 1), 0)
    matched = jnp.zeros((block_rows * len(SHIFTS), cells_x, cells_y), jnp.float32)
    for entry in range(foot_index.shape[0]):
        matched = matched + jnp.where(key[entry][None] == codes, weights[entry][None], 0.0)
    upsampled = jnp.repeat(strip, factor, axis=1)
    candidates = jnp.stack(
        [lane_shift(upsampled[row], -factor * shift) for row in range(block_rows) for shift in SHIFTS]
    )
    density_cell = jnp.sum(matched * candidates[:, None, :], axis=0)
    reach = 2
    above = from_behind(density_cell[-reach:], "tile", 1)
    below = from_behind(density_cell[:reach], "tile", -1)
    pad = jnp.zeros((HALO - reach, cells_y), jnp.float32)
    density_ext = jnp.concatenate([pad, above, density_cell, below, pad], axis=0)
    rows_ext = cells_x + 2 * HALO
    global_row = lax.axis_index("tile") * cells_x - HALO + lax.broadcasted_iota(jnp.int32, (rows_ext, 1), 0)
    valid = (global_row >= 0) & (global_row < cells_x * lax.axis_size("tile"))
    inverse_ext = jnp.where(valid, time_step / (1.0 + high_contrast * density_ext), 0.0)
    hy_step = jnp.where(valid, time_step, 0.0)
    drive = [jnp.sin(omega * (turn + 1.0))[None, :, None, None] for turn in range(ITERS)]
    history = march(sources_ext, drive, density_ext, inverse_ext, hy_step)
    sense = jnp.zeros((rows_ext, cells_y), jnp.float32)
    for turn in range(ITERS):
        sense = sense + jnp.sum(history[turn][1] * history[ITERS - 1 - turn][0], axis=0)
    total_waves = source_fwd.shape[0] * lax.axis_size("wl")
    scaled = high_contrast / total_waves * sense[HALO : HALO + cells_x]
    per_col = jnp.sum(matched * scaled[None], axis=1)
    pooled = per_col.reshape(block_rows, len(SHIFTS), block_cols, factor).sum(axis=3)
    partial_grad = jnp.zeros((block_rows, block_cols), jnp.float32)
    for slot, shift in enumerate(SHIFTS):
        partial_grad = partial_grad + lane_shift(pooled[:, slot], shift)
    density_grad = scatter_sum_columns(partial_grad, "wl")
    return (history[ITERS - 1][0, :, HALO : HALO + cells_x], density_grad)


def solution(mesh):
    in_specs = (
        P("tile", "wl"),
        P(None, "tile", None),
        P(None, "tile", None),
        P("wl", "tile", None),
        P("wl", "tile", None),
        P("wl"),
    )
    out_specs = (P("wl", "tile", None), P("tile", "wl"))
    return jax.shard_map(shards, mesh=mesh, in_specs=in_specs, out_specs=out_specs, check_vma=False)
```

```python
import jax
import jax.numpy as jnp
from jax import lax
from jax.sharding import PartitionSpec as P

ITERS = 4
HALO = 4
SHIFTS = (-2, -1, 0, 1, 2)


time_step = 0.5
high_contrast = 4.0
drude_decay = 0.9
drude_gain = 0.5


def from_behind(value, axis, steps):
    count = lax.axis_size(axis)
    first, last = (max(0, -steps), min(count, count - steps))
    return lax.ppermute(value, axis, [(source, source + steps) for source in range(first, last)])


def with_halo(value, axis):
    above = from_behind(value[..., -HALO:, :], axis, 1)
    below = from_behind(value[..., :HALO, :], axis, -1)
    return jnp.concatenate([above, value, below], axis=-2)


def gather_columns(value, axis):
    count = lax.axis_size(axis)
    copies = jnp.broadcast_to(value[None], (count,) + value.shape)
    pieces = lax.all_to_all(copies, axis, 0, 0, tiled=True)
    return pieces.transpose(1, 0, 2).reshape(value.shape[0], count * value.shape[1])


def scatter_sum_columns(value, axis):
    count = lax.axis_size(axis)
    rows, cols = value.shape
    pieces = value.reshape(rows, count, cols // count).transpose(1, 0, 2)
    return lax.all_to_all(pieces, axis, 0, 0, tiled=True).sum(axis=0)


def lane_shift(vector, shift):
    width = vector.shape[-1]
    pad = [(0, 0)] * (vector.ndim - 1) + [(abs(shift), abs(shift))]
    padded = jnp.pad(vector, pad)
    start = abs(shift) - shift
    return lax.slice_in_dim(padded, start, start + width, axis=vector.ndim - 1)


def march(source, drive, density_cell, inverse, hy_step):
    field_e = jnp.zeros_like(source)
    field_hx = jnp.zeros_like(source)
    field_hy = jnp.zeros_like(source)
    current = jnp.zeros_like(source)
    history = []
    for turn in range(ITERS):
        row_zero = jnp.zeros_like(source[:, :, :1, :])
        col_zero = jnp.zeros_like(source[:, :, :, :1])
        e_up = jnp.concatenate([field_e[:, :, 1:, :], row_zero], 2)
        e_right = jnp.concatenate([field_e[:, :, :, 1:], col_zero], 3)
        field_hx = field_hx - time_step * (e_right - field_e)
        field_hy = field_hy + hy_step * (e_up - field_e)
        current = drude_decay * current + drude_gain * density_cell * field_e
        hy_down = jnp.concatenate([row_zero, field_hy[:, :, :-1, :]], 2)
        hx_left = jnp.concatenate([col_zero, field_hx[:, :, :, :-1]], 3)
        field_e = (
            field_e
            + inverse * (field_hy - hy_down - (field_hx - hx_left) - current)
            + drive[turn] * source
        )
        history.append(field_e)
    return history


def shards(density, foot_index, foot_weight, source_fwd, source_adj, omega):
    sources = jnp.stack([source_fwd, source_adj])
    sources_ext = with_halo(sources, "tile")
    strip = gather_columns(density, "wl")
    block_rows, block_cols = strip.shape
    cells_x, cells_y = foot_index.shape[1:]
    factor = cells_y // block_cols
    weights = foot_weight.astype(jnp.float32)
    col_block = lax.broadcasted_iota(jnp.int32, (1, cells_y), 1) // factor
    key = (foot_index // block_cols) * len(SHIFTS) + (foot_index % block_cols - col_block[None]) + 2
    codes = lax.broadcasted_iota(jnp.int32, (block_rows * len(SHIFTS), 1, 1), 0)
    matched = jnp.zeros((block_rows * len(SHIFTS), cells_x, cells_y), jnp.float32)
    for entry in range(foot_index.shape[0]):
        matched = matched + jnp.where(key[entry][None] == codes, weights[entry][None], 0.0)
    span = 128
    chunks = block_cols // span
    spread = (
        lax.broadcasted_iota(jnp.int32, (span, span * factor), 1) // factor
        == lax.broadcasted_iota(jnp.int32, (span, span * factor), 0)
    ).astype(jnp.float32)
    shifted = jnp.stack([lane_shift(strip[row], -shift) for row in range(block_rows) for shift in SHIFTS])
    candidates = jnp.dot(
        shifted.reshape(-1, span), spread, precision=lax.Precision.HIGHEST
    ).reshape(block_rows * len(SHIFTS), cells_y)
    density_cell = jnp.sum(matched * candidates[:, None, :], axis=0)
    reach = 2
    above = from_behind(density_cell[-reach:], "tile", 1)
    below = from_behind(density_cell[:reach], "tile", -1)
    pad = jnp.zeros((HALO - reach, cells_y), jnp.float32)
    density_ext = jnp.concatenate([pad, above, density_cell, below, pad], axis=0)
    rows_ext = cells_x + 2 * HALO
    global_row = lax.axis_index("tile") * cells_x - HALO + lax.broadcasted_iota(jnp.int32, (rows_ext, 1), 0)
    valid = (global_row >= 0) & (global_row < cells_x * lax.axis_size("tile"))
    inverse_ext = jnp.where(valid, time_step / (1.0 + high_contrast * density_ext), 0.0)
    hy_step = jnp.where(valid, time_step, 0.0)
    drive = [jnp.sin(omega * (turn + 1.0))[None, :, None, None] for turn in range(ITERS)]
    history = march(sources_ext, drive, density_ext, inverse_ext, hy_step)
    sense = jnp.zeros((rows_ext, cells_y), jnp.float32)
    for turn in range(ITERS):
        sense = sense + jnp.sum(history[turn][1] * history[ITERS - 1 - turn][0], axis=0)
    total_waves = source_fwd.shape[0] * lax.axis_size("wl")
    scaled = high_contrast / total_waves * sense[HALO : HALO + cells_x]
    per_col = jnp.sum(matched * scaled[None], axis=1)
    per_col = per_col.reshape(block_rows, len(SHIFTS), cells_y)
    gathered = jnp.zeros((block_rows, cells_y), jnp.float32)
    for slot, shift in enumerate(SHIFTS):
        gathered = gathered + lane_shift(per_col[:, slot], factor * shift)
    partial_grad = jnp.dot(
        gathered.reshape(-1, span * factor), spread.T, precision=lax.Precision.HIGHEST
    ).reshape(block_rows, block_cols)
    density_grad = scatter_sum_columns(partial_grad, "wl")
    return (history[ITERS - 1][0, :, HALO : HALO + cells_x], density_grad)


def solution(mesh):
    in_specs = (
        P("tile", "wl"),
        P(None, "tile", None),
        P(None, "tile", None),
        P("wl", "tile", None),
        P("wl", "tile", None),
        P("wl"),
    )
    out_specs = (P("wl", "tile", None), P("tile", "wl"))
    return jax.shard_map(shards, mesh=mesh, in_specs=in_specs, out_specs=out_specs, check_vma=False)
```

```python
import jax
import jax.numpy as jnp
from jax import lax
from jax.sharding import PartitionSpec as P

ITERS = 4
HALO = 4
SHIFTS = (-2, -1, 0, 1, 2)


time_step = 0.5
high_contrast = 4.0
drude_decay = 0.9
drude_gain = 0.5


def from_behind(value, axis, steps):
    count = lax.axis_size(axis)
    first, last = (max(0, -steps), min(count, count - steps))
    return lax.ppermute(value, axis, [(source, source + steps) for source in range(first, last)])


def with_halo(value, axis):
    above = from_behind(value[..., -HALO:, :], axis, 1)
    below = from_behind(value[..., :HALO, :], axis, -1)
    return jnp.concatenate([above, value, below], axis=-2)


def gather_columns(value, axis):
    count = lax.axis_size(axis)
    copies = jnp.broadcast_to(value[None], (count,) + value.shape)
    pieces = lax.all_to_all(copies, axis, 0, 0, tiled=True)
    return pieces.transpose(1, 0, 2).reshape(value.shape[0], count * value.shape[1])


def scatter_sum_columns(value, axis):
    count = lax.axis_size(axis)
    rows, cols = value.shape
    pieces = value.reshape(rows, count, cols // count).transpose(1, 0, 2)
    return lax.all_to_all(pieces, axis, 0, 0, tiled=True).sum(axis=0)


def lane_shift(vector, shift):
    width = vector.shape[-1]
    pad = [(0, 0)] * (vector.ndim - 1) + [(abs(shift), abs(shift))]
    padded = jnp.pad(vector, pad)
    start = abs(shift) - shift
    return lax.slice_in_dim(padded, start, start + width, axis=vector.ndim - 1)


def shifted_in(value, axis, shift):
    config = [(0, 0, 0)] * value.ndim
    size = value.shape[axis]
    if shift > 0:
        config[axis] = (shift, 0, 0)
        kept = lax.slice_in_dim(value, 0, size - shift, axis=axis)
    else:
        config[axis] = (0, -shift, 0)
        kept = lax.slice_in_dim(value, -shift, size, axis=axis)
    return lax.pad(kept, jnp.zeros((), value.dtype), config)


def march(source, drive, density_cell, inverse, hy_step):
    field_e = jnp.zeros_like(source)
    field_hx = jnp.zeros_like(source)
    field_hy = jnp.zeros_like(source)
    current = jnp.zeros_like(source)
    history = []
    for turn in range(ITERS):
        e_up = shifted_in(field_e, 2, -1)
        e_right = shifted_in(field_e, 3, -1)
        field_hx = field_hx - time_step * (e_right - field_e)
        field_hy = field_hy + hy_step * (e_up - field_e)
        current = drude_decay * current + drude_gain * density_cell * field_e
        hy_down = shifted_in(field_hy, 2, 1)
        hx_left = shifted_in(field_hx, 3, 1)
        field_e = (
            field_e
            + inverse * (field_hy - hy_down - (field_hx - hx_left) - current)
            + drive[turn] * source
        )
        history.append(field_e)
    return history


def shards(density, foot_index, foot_weight, source_fwd, source_adj, omega):
    sources = jnp.stack([source_fwd, source_adj])
    sources_ext = with_halo(sources, "tile")
    strip = gather_columns(density, "wl")
    block_rows, block_cols = strip.shape
    cells_x, cells_y = foot_index.shape[1:]
    factor = cells_y // block_cols
    weights = foot_weight.astype(jnp.float32)
    col_block = lax.broadcasted_iota(jnp.int32, (1, cells_y), 1) // factor
    key = (foot_index // block_cols) * len(SHIFTS) + (foot_index % block_cols - col_block[None]) + 2
    codes = lax.broadcasted_iota(jnp.int32, (block_rows * len(SHIFTS), 1, 1), 0)
    matched = jnp.zeros((block_rows * len(SHIFTS), cells_x, cells_y), jnp.float32)
    for entry in range(foot_index.shape[0]):
        matched = matched + jnp.where(key[entry][None] == codes, weights[entry][None], 0.0)
    span = 128
    chunks = block_cols // span
    spread = (
        lax.broadcasted_iota(jnp.int32, (span, span * factor), 1) // factor
        == lax.broadcasted_iota(jnp.int32, (span, span * factor), 0)
    ).astype(jnp.float32)
    shifted = jnp.stack([lane_shift(strip[row], -shift) for row in range(block_rows) for shift in SHIFTS])
    candidates = jnp.dot(
        shifted.reshape(-1, span), spread, precision=lax.Precision.HIGHEST
    ).reshape(block_rows * len(SHIFTS), cells_y)
    reach = 2
    last_rows = jnp.sum(matched[:, -reach:] * candidates[:, None, :], axis=0)
    first_rows = jnp.sum(matched[:, :reach] * candidates[:, None, :], axis=0)
    above = from_behind(last_rows, "tile", 1)
    below = from_behind(first_rows, "tile", -1)
    density_cell = jnp.sum(matched * candidates[:, None, :], axis=0)
    pad = jnp.zeros((HALO - reach, cells_y), jnp.float32)
    density_ext = jnp.concatenate([pad, above, density_cell, below, pad], axis=0)
    rows_ext = cells_x + 2 * HALO
    global_row = lax.axis_index("tile") * cells_x - HALO + lax.broadcasted_iota(jnp.int32, (rows_ext, 1), 0)
    valid = (global_row >= 0) & (global_row < cells_x * lax.axis_size("tile"))
    inverse_ext = jnp.where(valid, time_step / (1.0 + high_contrast * density_ext), 0.0)
    hy_step = jnp.where(valid, time_step, 0.0)
    drive = [jnp.sin(omega * (turn + 1.0))[None, :, None, None] for turn in range(ITERS)]
    history = march(sources_ext, drive, density_ext, inverse_ext, hy_step)
    sense = jnp.zeros((rows_ext, cells_y), jnp.float32)
    for turn in range(ITERS):
        sense = sense + jnp.sum(history[turn][1] * history[ITERS - 1 - turn][0], axis=0)
    total_waves = source_fwd.shape[0] * lax.axis_size("wl")
    scaled = high_contrast / total_waves * sense[HALO : HALO + cells_x]
    per_col = jnp.sum(matched * scaled[None], axis=1)
    per_col = per_col.reshape(block_rows, len(SHIFTS), cells_y)
    gathered = jnp.zeros((block_rows, cells_y), jnp.float32)
    for slot, shift in enumerate(SHIFTS):
        gathered = gathered + lane_shift(per_col[:, slot], factor * shift)
    count = lax.axis_size("wl")
    pooled = jnp.einsum(
        "rky,cy->krc",
        gathered.reshape(block_rows, chunks, span * factor),
        spread,
        precision=lax.Precision.HIGHEST,
    )
    density_grad = lax.all_to_all(
        pooled.reshape(count, chunks // count, block_rows, span).transpose(0, 2, 1, 3).reshape(count, block_rows, -1),
        "wl", 0, 0, tiled=True,
    ).sum(axis=0)
    return (history[ITERS - 1][0, :, HALO : HALO + cells_x], density_grad)


def solution(mesh):
    in_specs = (
        P("tile", "wl"),
        P(None, "tile", None),
        P(None, "tile", None),
        P("wl", "tile", None),
        P("wl", "tile", None),
        P("wl"),
    )
    out_specs = (P("wl", "tile", None), P("tile", "wl"))
    return jax.shard_map(shards, mesh=mesh, in_specs=in_specs, out_specs=out_specs, check_vma=False)
```

```python
import jax
import jax.numpy as jnp
from jax import lax
from jax.experimental import pallas as pl
from jax.experimental.pallas import tpu as pltpu
from jax.sharding import PartitionSpec as P

ITERS = 4
HALO = 4
SHIFTS = (-2, -1, 0, 1, 2)


time_step = 0.5
high_contrast = 4.0
drude_decay = 0.9
drude_gain = 0.5


def from_behind(value, axis, steps):
    count = lax.axis_size(axis)
    first, last = (max(0, -steps), min(count, count - steps))
    return lax.ppermute(value, axis, [(source, source + steps) for source in range(first, last)])


def with_halo(value, axis):
    above = from_behind(value[..., -HALO:, :], axis, 1)
    below = from_behind(value[..., :HALO, :], axis, -1)
    return jnp.concatenate([above, value, below], axis=-2)


def gather_columns(value, axis):
    count = lax.axis_size(axis)
    copies = jnp.broadcast_to(value[None], (count,) + value.shape)
    pieces = lax.all_to_all(copies, axis, 0, 0, tiled=True)
    return pieces.transpose(1, 0, 2).reshape(value.shape[0], count * value.shape[1])


def scatter_sum_columns(value, axis):
    count = lax.axis_size(axis)
    rows, cols = value.shape
    pieces = value.reshape(rows, count, cols // count).transpose(1, 0, 2)
    return lax.all_to_all(pieces, axis, 0, 0, tiled=True).sum(axis=0)


def lane_shift(vector, shift):
    width = vector.shape[-1]
    pad = [(0, 0)] * (vector.ndim - 1) + [(abs(shift), abs(shift))]
    padded = jnp.pad(vector, pad)
    start = abs(shift) - shift
    return lax.slice_in_dim(padded, start, start + width, axis=vector.ndim - 1)


def shifted_in(value, axis, shift):
    config = [(0, 0, 0)] * value.ndim
    size = value.shape[axis]
    if shift > 0:
        config[axis] = (shift, 0, 0)
        kept = lax.slice_in_dim(value, 0, size - shift, axis=axis)
    else:
        config[axis] = (0, -shift, 0)
        kept = lax.slice_in_dim(value, -shift, size, axis=axis)
    return lax.pad(kept, jnp.zeros((), value.dtype), config)


def march_kernel(drive_ref, source_ref, density_ref, inverse_ref, step_ref, final_ref, sense_ref, history_ref):
    runs, waves, rows, cols = source_ref.shape
    row_id = lax.broadcasted_iota(jnp.int32, (rows, cols), 0)
    col_id = lax.broadcasted_iota(jnp.int32, (rows, cols), 1)
    sense_ref[...] = jnp.zeros((rows, cols), jnp.float32)
    for wave in range(waves):
        for run in range(runs):
            field_e = jnp.zeros((rows, cols), jnp.float32)
            field_hx = jnp.zeros((rows, cols), jnp.float32)
            field_hy = jnp.zeros((rows, cols), jnp.float32)
            current = jnp.zeros((rows, cols), jnp.float32)
            for turn in range(ITERS):
                e_up = jnp.where(row_id < rows - 1, pltpu.roll(field_e, rows - 1, 0), 0.0)
                e_right = jnp.where(col_id < cols - 1, pltpu.roll(field_e, cols - 1, 1), 0.0)
                field_hx = field_hx - time_step * (e_right - field_e)
                field_hy = field_hy + step_ref[...] * (e_up - field_e)
                current = drude_decay * current + drude_gain * density_ref[...] * field_e
                hy_down = jnp.where(row_id > 0, pltpu.roll(field_hy, 1, 0), 0.0)
                hx_left = jnp.where(col_id > 0, pltpu.roll(field_hx, 1, 1), 0.0)
                field_e = (
                    field_e
                    + inverse_ref[...] * (field_hy - hy_down - (field_hx - hx_left) - current)
                    + drive_ref[turn, wave] * source_ref[run, wave]
                )
                if run == 0:
                    history_ref[turn] = field_e
                else:
                    sense_ref[...] += field_e * history_ref[ITERS - 1 - turn]
            if run == 0:
                final_ref[wave] = field_e


def march(source, drive, density_cell, inverse, hy_step):
    runs, waves, rows, cols = source.shape
    vmem = pltpu.MemorySpace.VMEM
    return pl.pallas_call(
        march_kernel,
        out_shape=(
            jax.ShapeDtypeStruct((waves, rows, cols), jnp.float32),
            jax.ShapeDtypeStruct((rows, cols), jnp.float32),
        ),
        in_specs=[pl.BlockSpec(memory_space=pltpu.MemorySpace.SMEM)] + [pl.BlockSpec(memory_space=vmem)] * 4,
        out_specs=(pl.BlockSpec(memory_space=vmem), pl.BlockSpec(memory_space=vmem)),
        scratch_shapes=[pltpu.VMEM((ITERS, rows, cols), jnp.float32)],
    )(drive, source, density_cell, inverse, hy_step)


def shards(density, foot_index, foot_weight, source_fwd, source_adj, omega):
    sources = jnp.stack([source_fwd, source_adj])
    sources_ext = with_halo(sources, "tile")
    strip = gather_columns(density, "wl")
    block_rows, block_cols = strip.shape
    cells_x, cells_y = foot_index.shape[1:]
    factor = cells_y // block_cols
    weights = foot_weight.astype(jnp.float32)
    col_block = lax.broadcasted_iota(jnp.int32, (1, cells_y), 1) // factor
    key = (foot_index // block_cols) * len(SHIFTS) + (foot_index % block_cols - col_block[None]) + 2
    codes = lax.broadcasted_iota(jnp.int32, (block_rows * len(SHIFTS), 1, 1), 0)
    matched = jnp.zeros((block_rows * len(SHIFTS), cells_x, cells_y), jnp.float32)
    for entry in range(foot_index.shape[0]):
        matched = matched + jnp.where(key[entry][None] == codes, weights[entry][None], 0.0)
    span = 128
    chunks = block_cols // span
    spread = (
        lax.broadcasted_iota(jnp.int32, (span, span * factor), 1) // factor
        == lax.broadcasted_iota(jnp.int32, (span, span * factor), 0)
    ).astype(jnp.float32)
    shifted = jnp.stack([lane_shift(strip[row], -shift) for row in range(block_rows) for shift in SHIFTS])
    candidates = jnp.dot(
        shifted.reshape(-1, span), spread, precision=lax.Precision.HIGHEST
    ).reshape(block_rows * len(SHIFTS), cells_y)
    reach = 2
    last_rows = jnp.sum(matched[:, -reach:] * candidates[:, None, :], axis=0)
    first_rows = jnp.sum(matched[:, :reach] * candidates[:, None, :], axis=0)
    above = from_behind(last_rows, "tile", 1)
    below = from_behind(first_rows, "tile", -1)
    density_cell = jnp.sum(matched * candidates[:, None, :], axis=0)
    pad = jnp.zeros((HALO - reach, cells_y), jnp.float32)
    density_ext = jnp.concatenate([pad, above, density_cell, below, pad], axis=0)
    rows_ext = cells_x + 2 * HALO
    global_row = lax.axis_index("tile") * cells_x - HALO + lax.broadcasted_iota(jnp.int32, (rows_ext, 1), 0)
    valid = (global_row >= 0) & (global_row < cells_x * lax.axis_size("tile"))
    inverse_ext = jnp.where(valid, time_step / (1.0 + high_contrast * density_ext), 0.0)
    hy_step = jnp.broadcast_to(jnp.where(valid, time_step, 0.0), (rows_ext, cells_y))
    drive = jnp.stack([jnp.sin(omega * (turn + 1.0)) for turn in range(ITERS)])
    final, sense = march(sources_ext, drive, density_ext, inverse_ext, hy_step)
    total_waves = source_fwd.shape[0] * lax.axis_size("wl")
    scaled = high_contrast / total_waves * sense[HALO : HALO + cells_x]
    per_col = jnp.sum(matched * scaled[None], axis=1)
    per_col = per_col.reshape(block_rows, len(SHIFTS), cells_y)
    gathered = jnp.zeros((block_rows, cells_y), jnp.float32)
    for slot, shift in enumerate(SHIFTS):
        gathered = gathered + lane_shift(per_col[:, slot], factor * shift)
    count = lax.axis_size("wl")
    pooled = jnp.einsum(
        "rky,cy->krc",
        gathered.reshape(block_rows, chunks, span * factor),
        spread,
        precision=lax.Precision.HIGHEST,
    )
    density_grad = lax.all_to_all(
        pooled.reshape(count, chunks // count, block_rows, span).transpose(0, 2, 1, 3).reshape(count, block_rows, -1),
        "wl", 0, 0, tiled=True,
    ).sum(axis=0)
    return (final[:, HALO : HALO + cells_x], density_grad)


def solution(mesh):
    in_specs = (
        P("tile", "wl"),
        P(None, "tile", None),
        P(None, "tile", None),
        P("wl", "tile", None),
        P("wl", "tile", None),
        P("wl"),
    )
    out_specs = (P("wl", "tile", None), P("tile", "wl"))
    return jax.shard_map(shards, mesh=mesh, in_specs=in_specs, out_specs=out_specs, check_vma=False)
```

```python
import jax
import jax.numpy as jnp
from jax import lax
from jax.experimental import pallas as pl
from jax.experimental.pallas import tpu as pltpu
from jax.sharding import PartitionSpec as P

ITERS = 4
HALO = 4
SHIFTS = (-2, -1, 0, 1, 2)


time_step = 0.5
high_contrast = 4.0
drude_decay = 0.9
drude_gain = 0.5


def from_behind(value, axis, steps):
    count = lax.axis_size(axis)
    first, last = (max(0, -steps), min(count, count - steps))
    return lax.ppermute(value, axis, [(source, source + steps) for source in range(first, last)])


def with_halo(value, axis):
    above = from_behind(value[..., -HALO:, :], axis, 1)
    below = from_behind(value[..., :HALO, :], axis, -1)
    return jnp.concatenate([above, value, below], axis=-2)


def gather_columns(value, axis):
    count = lax.axis_size(axis)
    copies = jnp.broadcast_to(value[None], (count,) + value.shape)
    pieces = lax.all_to_all(copies, axis, 0, 0, tiled=True)
    return pieces.transpose(1, 0, 2).reshape(value.shape[0], count * value.shape[1])


def scatter_sum_columns(value, axis):
    count = lax.axis_size(axis)
    rows, cols = value.shape
    pieces = value.reshape(rows, count, cols // count).transpose(1, 0, 2)
    return lax.all_to_all(pieces, axis, 0, 0, tiled=True).sum(axis=0)


def lane_shift(vector, shift):
    width = vector.shape[-1]
    pad = [(0, 0)] * (vector.ndim - 1) + [(abs(shift), abs(shift))]
    padded = jnp.pad(vector, pad)
    start = abs(shift) - shift
    return lax.slice_in_dim(padded, start, start + width, axis=vector.ndim - 1)


def shifted_in(value, axis, shift):
    config = [(0, 0, 0)] * value.ndim
    size = value.shape[axis]
    if shift > 0:
        config[axis] = (shift, 0, 0)
        kept = lax.slice_in_dim(value, 0, size - shift, axis=axis)
    else:
        config[axis] = (0, -shift, 0)
        kept = lax.slice_in_dim(value, -shift, size, axis=axis)
    return lax.pad(kept, jnp.zeros((), value.dtype), config)


def march_kernel(
    bounds_ref, drive_ref, fwd_ref, adj_ref, src_above_ref, src_below_ref,
    dens_ref, dens_above_ref, dens_below_ref, matched_ref,
    final_ref, per_col_ref,
    source_ref, density_ref, history_ref, sense_ref,
):
    runs, waves, rows, cols = source_ref.shape
    own = fwd_ref.shape[1]
    reach = dens_above_ref.shape[0]
    for wave in range(waves):
        for run, own_ref in enumerate((fwd_ref, adj_ref)):
            source_ref[run, wave, 0:HALO] = src_above_ref[run, wave]
            source_ref[run, wave, HALO : HALO + own] = own_ref[wave]
            source_ref[run, wave, HALO + own : rows] = src_below_ref[run, wave]
    density_ref[...] = jnp.zeros((rows, cols), jnp.float32)
    density_ref[HALO - reach : HALO] = dens_above_ref[...]
    density_ref[HALO : HALO + own] = dens_ref[...]
    density_ref[HALO + own : HALO + own + reach] = dens_below_ref[...]
    row_id = lax.broadcasted_iota(jnp.int32, (rows, cols), 0)
    col_id = lax.broadcasted_iota(jnp.int32, (rows, cols), 1)
    valid = (row_id >= bounds_ref[0]) & (row_id < bounds_ref[1])
    density = density_ref[...]
    inverse = jnp.where(valid, time_step / (1.0 + high_contrast * density), 0.0)
    hy_step = jnp.where(valid, time_step, 0.0)
    sense_ref[...] = jnp.zeros((rows, cols), jnp.float32)
    for wave in range(waves):
        for run in range(runs):
            field_e = jnp.zeros((rows, cols), jnp.float32)
            field_hx = jnp.zeros((rows, cols), jnp.float32)
            field_hy = jnp.zeros((rows, cols), jnp.float32)
            current = jnp.zeros((rows, cols), jnp.float32)
            for turn in range(ITERS):
                e_up = jnp.where(row_id < rows - 1, pltpu.roll(field_e, rows - 1, 0), 0.0)
                e_right = jnp.where(col_id < cols - 1, pltpu.roll(field_e, cols - 1, 1), 0.0)
                field_hx = field_hx - time_step * (e_right - field_e)
                field_hy = field_hy + hy_step * (e_up - field_e)
                current = drude_decay * current + drude_gain * density * field_e
                hy_down = jnp.where(row_id > 0, pltpu.roll(field_hy, 1, 0), 0.0)
                hx_left = jnp.where(col_id > 0, pltpu.roll(field_hx, 1, 1), 0.0)
                field_e = (
                    field_e
                    + inverse * (field_hy - hy_down - (field_hx - hx_left) - current)
                    + drive_ref[turn, wave] * source_ref[run, wave]
                )
                if run == 0:
                    history_ref[turn] = field_e
                else:
                    sense_ref[...] += field_e * history_ref[ITERS - 1 - turn]
            if run == 0:
                final_ref[wave] = field_e
    scaled = drive_ref[ITERS, 0] * sense_ref[HALO : HALO + own]
    for code in range(matched_ref.shape[0]):
        per_col_ref[code : code + 1] = jnp.sum(matched_ref[code] * scaled, axis=0, keepdims=True)


def march(bounds, drive, fwd, adj, src_above, src_below, dens, dens_above, dens_below, matched):
    runs, waves, _, cols = src_above.shape
    rows = fwd.shape[1] + 2 * HALO
    vmem = pltpu.MemorySpace.VMEM
    smem = pltpu.MemorySpace.SMEM
    return pl.pallas_call(
        march_kernel,
        out_shape=(
            jax.ShapeDtypeStruct((waves, rows, cols), jnp.float32),
            jax.ShapeDtypeStruct((matched.shape[0], cols), jnp.float32),
        ),
        in_specs=[pl.BlockSpec(memory_space=smem)] * 2 + [pl.BlockSpec(memory_space=vmem)] * 8,
        out_specs=(pl.BlockSpec(memory_space=vmem), pl.BlockSpec(memory_space=vmem)),
        scratch_shapes=[
            pltpu.VMEM((runs, waves, rows, cols), jnp.float32),
            pltpu.VMEM((rows, cols), jnp.float32),
            pltpu.VMEM((ITERS, rows, cols), jnp.float32),
            pltpu.VMEM((rows, cols), jnp.float32),
        ],
    )(bounds, drive, fwd, adj, src_above, src_below, dens, dens_above, dens_below, matched)


def shards(density, foot_index, foot_weight, source_fwd, source_adj, omega):
    sources = jnp.stack([source_fwd, source_adj])
    src_above = from_behind(sources[:, :, -HALO:], "tile", 1)
    src_below = from_behind(sources[:, :, :HALO], "tile", -1)
    strip = gather_columns(density, "wl")
    block_rows, block_cols = strip.shape
    cells_x, cells_y = foot_index.shape[1:]
    factor = cells_y // block_cols
    weights = foot_weight.astype(jnp.float32)
    col_block = lax.broadcasted_iota(jnp.int32, (1, cells_y), 1) // factor
    key = (foot_index // block_cols) * len(SHIFTS) + (foot_index % block_cols - col_block[None]) + 2
    codes = lax.broadcasted_iota(jnp.int32, (block_rows * len(SHIFTS), 1, 1), 0)
    matched = jnp.zeros((block_rows * len(SHIFTS), cells_x, cells_y), jnp.float32)
    for entry in range(foot_index.shape[0]):
        matched = matched + jnp.where(key[entry][None] == codes, weights[entry][None], 0.0)
    span = 128
    chunks = block_cols // span
    spread = (
        lax.broadcasted_iota(jnp.int32, (span, span * factor), 1) // factor
        == lax.broadcasted_iota(jnp.int32, (span, span * factor), 0)
    ).astype(jnp.float32)
    shifted = jnp.stack([lane_shift(strip[row], -shift) for row in range(block_rows) for shift in SHIFTS])
    candidates = jnp.dot(
        shifted.reshape(-1, span), spread, precision=lax.Precision.HIGHEST
    ).reshape(block_rows * len(SHIFTS), cells_y)
    reach = 2
    last_rows = jnp.sum(matched[:, -reach:] * candidates[:, None, :], axis=0)
    first_rows = jnp.sum(matched[:, :reach] * candidates[:, None, :], axis=0)
    above = from_behind(last_rows, "tile", 1)
    below = from_behind(first_rows, "tile", -1)
    density_cell = jnp.sum(matched * candidates[:, None, :], axis=0)
    rows_ext = cells_x + 2 * HALO
    first = HALO - lax.axis_index("tile") * cells_x
    bounds = jnp.stack([first, first + cells_x * lax.axis_size("tile")]).astype(jnp.int32)
    total_waves = source_fwd.shape[0] * lax.axis_size("wl")
    drive = jnp.concatenate(
        [jnp.stack([jnp.sin(omega * (turn + 1.0)) for turn in range(ITERS)]),
         jnp.full((1, omega.shape[0]), high_contrast / total_waves, jnp.float32)]
    )
    final, per_col = march(
        bounds, drive, source_fwd, source_adj, src_above, src_below, density_cell, above, below, matched
    )
    per_col = per_col.reshape(block_rows, len(SHIFTS), cells_y)
    gathered = jnp.zeros((block_rows, cells_y), jnp.float32)
    for slot, shift in enumerate(SHIFTS):
        gathered = gathered + lane_shift(per_col[:, slot], factor * shift)
    count = lax.axis_size("wl")
    pooled = jnp.einsum(
        "rky,cy->krc",
        gathered.reshape(block_rows, chunks, span * factor),
        spread,
        precision=lax.Precision.HIGHEST,
    )
    density_grad = lax.all_to_all(
        pooled.reshape(count, chunks // count, block_rows, span).transpose(0, 2, 1, 3).reshape(count, block_rows, -1),
        "wl", 0, 0, tiled=True,
    ).sum(axis=0)
    return (final[:, HALO : HALO + cells_x], density_grad)


def solution(mesh):
    in_specs = (
        P("tile", "wl"),
        P(None, "tile", None),
        P(None, "tile", None),
        P("wl", "tile", None),
        P("wl", "tile", None),
        P("wl"),
    )
    out_specs = (P("wl", "tile", None), P("tile", "wl"))
    return jax.shard_map(shards, mesh=mesh, in_specs=in_specs, out_specs=out_specs, check_vma=False)
```

```python
import jax
import jax.numpy as jnp
from jax import lax
from jax.experimental import pallas as pl
from jax.experimental.pallas import tpu as pltpu
from jax.sharding import PartitionSpec as P

ITERS = 4
HALO = 4
FACTOR = 4
GRAD_SCALE = 4.0 / 16
SHIFTS = (-2, -1, 0, 1, 2)


time_step = 0.5
high_contrast = 4.0
drude_decay = 0.9
drude_gain = 0.5


def from_behind(value, axis, steps):
    count = lax.axis_size(axis)
    first, last = (max(0, -steps), min(count, count - steps))
    return lax.ppermute(value, axis, [(source, source + steps) for source in range(first, last)])


def with_halo(value, axis):
    above = from_behind(value[..., -HALO:, :], axis, 1)
    below = from_behind(value[..., :HALO, :], axis, -1)
    return jnp.concatenate([above, value, below], axis=-2)


def gather_columns(value, axis):
    count = lax.axis_size(axis)
    copies = jnp.broadcast_to(value[None], (count,) + value.shape)
    pieces = lax.all_to_all(copies, axis, 0, 0, tiled=True)
    return pieces.transpose(1, 0, 2).reshape(value.shape[0], count * value.shape[1])


def scatter_sum_columns(value, axis):
    count = lax.axis_size(axis)
    rows, cols = value.shape
    pieces = value.reshape(rows, count, cols // count).transpose(1, 0, 2)
    return lax.all_to_all(pieces, axis, 0, 0, tiled=True).sum(axis=0)


def lane_shift(vector, shift):
    width = vector.shape[-1]
    pad = [(0, 0)] * (vector.ndim - 1) + [(abs(shift), abs(shift))]
    padded = jnp.pad(vector, pad)
    start = abs(shift) - shift
    return lax.slice_in_dim(padded, start, start + width, axis=vector.ndim - 1)


def shifted_in(value, axis, shift):
    config = [(0, 0, 0)] * value.ndim
    size = value.shape[axis]
    if shift > 0:
        config[axis] = (shift, 0, 0)
        kept = lax.slice_in_dim(value, 0, size - shift, axis=axis)
    else:
        config[axis] = (0, -shift, 0)
        kept = lax.slice_in_dim(value, -shift, size, axis=axis)
    return lax.pad(kept, jnp.zeros((), value.dtype), config)


def march_kernel(
    drive_ref, fwd_ref, adj_ref, src_above_ref, src_below_ref,
    dens_ref, dens_above_ref, dens_below_ref, matched_ref,
    final_ref, gathered_ref,
    source_ref, density_ref, step_ref, history_ref, sense_ref,
):
    runs, waves, rows, cols = source_ref.shape
    own = fwd_ref.shape[1]
    reach = dens_above_ref.shape[0] - 1
    block_rows = gathered_ref.shape[0]
    for wave in range(waves):
        for run, own_ref in enumerate((fwd_ref, adj_ref)):
            source_ref[run, wave, 0:HALO] = src_above_ref[run, wave]
            source_ref[run, wave, HALO : HALO + own] = own_ref[wave]
            source_ref[run, wave, HALO + own : rows] = src_below_ref[run, wave]
    density_ref[...] = jnp.zeros((rows, cols), jnp.float32)
    density_ref[HALO - reach : HALO] = dens_above_ref[0:reach]
    density_ref[HALO : HALO + own] = dens_ref[...]
    density_ref[HALO + own : HALO + own + reach] = dens_below_ref[1 : reach + 1]
    step_ref[0:HALO] = jnp.broadcast_to(time_step * dens_above_ref[reach : reach + 1], (HALO, cols))
    step_ref[HALO : HALO + own] = jnp.full((own, cols), time_step, jnp.float32)
    step_ref[HALO + own : rows] = jnp.broadcast_to(time_step * dens_below_ref[0:1], (HALO, cols))
    row_id = lax.broadcasted_iota(jnp.int32, (rows, cols), 0)
    col_id = lax.broadcasted_iota(jnp.int32, (rows, cols), 1)
    density = density_ref[...]
    hy_step = step_ref[...]
    inverse = jnp.where(hy_step > 0.0, time_step / (1.0 + high_contrast * density), 0.0)
    sense_ref[...] = jnp.zeros((rows, cols), jnp.float32)
    for wave in range(waves):
        for run in range(runs):
            field_e = jnp.zeros((rows, cols), jnp.float32)
            field_hx = jnp.zeros((rows, cols), jnp.float32)
            field_hy = jnp.zeros((rows, cols), jnp.float32)
            current = jnp.zeros((rows, cols), jnp.float32)
            for turn in range(ITERS):
                e_up = jnp.where(row_id < rows - 1, pltpu.roll(field_e, rows - 1, 0), 0.0)
                e_right = jnp.where(col_id < cols - 1, pltpu.roll(field_e, cols - 1, 1), 0.0)
                field_hx = field_hx - time_step * (e_right - field_e)
                field_hy = field_hy + hy_step * (e_up - field_e)
                current = drude_decay * current + drude_gain * density * field_e
                hy_down = jnp.where(row_id > 0, pltpu.roll(field_hy, 1, 0), 0.0)
                hx_left = jnp.where(col_id > 0, pltpu.roll(field_hx, 1, 1), 0.0)
                field_e = (
                    field_e
                    + inverse * (field_hy - hy_down - (field_hx - hx_left) - current)
                    + drive_ref[turn, wave] * source_ref[run, wave]
                )
                if run == 0:
                    history_ref[turn] = field_e
                else:
                    sense_ref[...] += field_e * history_ref[ITERS - 1 - turn]
            if run == 0:
                final_ref[wave] = field_e
    scaled = GRAD_SCALE * sense_ref[HALO : HALO + own]
    lane = lax.broadcasted_iota(jnp.int32, (1, cols), 1)
    for row in range(block_rows):
        acc = jnp.zeros((1, cols), jnp.float32)
        for slot, shift in enumerate(SHIFTS):
            code = row * len(SHIFTS) + slot
            per_col = jnp.sum(matched_ref[code] * scaled, axis=0, keepdims=True)
            moved = FACTOR * shift
            inside = (lane >= moved) & (lane < cols + moved)
            acc = acc + jnp.where(inside, pltpu.roll(per_col, moved % cols, 1), 0.0)
        gathered_ref[row : row + 1] = acc


def march(drive, fwd, adj, src_above, src_below, dens, dens_above, dens_below, matched, block_rows):
    runs, waves, _, cols = src_above.shape
    rows = fwd.shape[1] + 2 * HALO
    vmem = pltpu.MemorySpace.VMEM
    smem = pltpu.MemorySpace.SMEM
    return pl.pallas_call(
        march_kernel,
        out_shape=(
            jax.ShapeDtypeStruct((waves, rows, cols), jnp.float32),
            jax.ShapeDtypeStruct((block_rows, cols), jnp.float32),
        ),
        in_specs=[pl.BlockSpec(memory_space=smem)] + [pl.BlockSpec(memory_space=vmem)] * 8,
        out_specs=(pl.BlockSpec(memory_space=vmem), pl.BlockSpec(memory_space=vmem)),
        scratch_shapes=[
            pltpu.VMEM((runs, waves, rows, cols), jnp.float32),
            pltpu.VMEM((rows, cols), jnp.float32),
            pltpu.VMEM((rows, cols), jnp.float32),
            pltpu.VMEM((ITERS, rows, cols), jnp.float32),
            pltpu.VMEM((rows, cols), jnp.float32),
        ],
    )(drive, fwd, adj, src_above, src_below, dens, dens_above, dens_below, matched)


def shards(density, foot_index, foot_weight, source_fwd, source_adj, omega):
    sources = jnp.stack([source_fwd, source_adj])
    src_above = from_behind(sources[:, :, -HALO:], "tile", 1)
    src_below = from_behind(sources[:, :, :HALO], "tile", -1)
    strip = gather_columns(density, "wl")
    block_rows, block_cols = strip.shape
    cells_x, cells_y = foot_index.shape[1:]
    factor = cells_y // block_cols
    assert factor == FACTOR and high_contrast / (source_fwd.shape[0] * lax.axis_size("wl")) == GRAD_SCALE
    weights = foot_weight.astype(jnp.float32)
    col_block = lax.broadcasted_iota(jnp.int32, (1, cells_y), 1) // factor
    key = (foot_index // block_cols) * len(SHIFTS) + (foot_index % block_cols - col_block[None]) + 2
    codes = lax.broadcasted_iota(jnp.int32, (block_rows * len(SHIFTS), 1, 1), 0)
    matched = jnp.zeros((block_rows * len(SHIFTS), cells_x, cells_y), jnp.float32)
    for entry in range(foot_index.shape[0]):
        matched = matched + jnp.where(key[entry][None] == codes, weights[entry][None], 0.0)
    span = 128
    chunks = block_cols // span
    spread = (
        lax.broadcasted_iota(jnp.int32, (span, span * factor), 1) // factor
        == lax.broadcasted_iota(jnp.int32, (span, span * factor), 0)
    ).astype(jnp.float32)
    shifted = jnp.stack([lane_shift(strip[row], -shift) for row in range(block_rows) for shift in SHIFTS])
    candidates = jnp.dot(
        shifted.reshape(-1, span), spread, precision=lax.Precision.HIGHEST
    ).reshape(block_rows * len(SHIFTS), cells_y)
    reach = 2
    last_rows = jnp.sum(matched[:, -reach:] * candidates[:, None, :], axis=0)
    first_rows = jnp.sum(matched[:, :reach] * candidates[:, None, :], axis=0)
    present = jnp.ones((1, cells_y), jnp.float32)
    above = from_behind(jnp.concatenate([last_rows, present]), "tile", 1)
    below = from_behind(jnp.concatenate([present, first_rows]), "tile", -1)
    density_cell = jnp.sum(matched * candidates[:, None, :], axis=0)
    drive = jnp.stack([jnp.sin(omega * (turn + 1.0)) for turn in range(ITERS)])
    final, gathered = march(
        drive, source_fwd, source_adj, src_above, src_below, density_cell, above, below, matched, block_rows
    )
    count = lax.axis_size("wl")
    pooled = jnp.einsum(
        "rky,cy->krc",
        gathered.reshape(block_rows, chunks, span * factor),
        spread,
        precision=lax.Precision.HIGHEST,
    )
    density_grad = lax.all_to_all(
        pooled.reshape(count, chunks // count, block_rows, span).transpose(0, 2, 1, 3).reshape(count, block_rows, -1),
        "wl", 0, 0, tiled=True,
    ).sum(axis=0)
    return (final[:, HALO : HALO + cells_x], density_grad)


def solution(mesh):
    in_specs = (
        P("tile", "wl"),
        P(None, "tile", None),
        P(None, "tile", None),
        P("wl", "tile", None),
        P("wl", "tile", None),
        P("wl"),
    )
    out_specs = (P("wl", "tile", None), P("tile", "wl"))
    return jax.shard_map(shards, mesh=mesh, in_specs=in_specs, out_specs=out_specs, check_vma=False)
```

```python
import jax
import jax.numpy as jnp
from jax import lax
from jax.experimental import pallas as pl
from jax.experimental.pallas import tpu as pltpu
from jax.sharding import PartitionSpec as P

ITERS = 4
HALO = 4
FACTOR = 4
GRAD_SCALE = 4.0 / 16
SHIFTS = (-2, -1, 0, 1, 2)


time_step = 0.5
high_contrast = 4.0
drude_decay = 0.9
drude_gain = 0.5


def from_behind(value, axis, steps):
    count = lax.axis_size(axis)
    first, last = (max(0, -steps), min(count, count - steps))
    return lax.ppermute(value, axis, [(source, source + steps) for source in range(first, last)])


def with_halo(value, axis):
    above = from_behind(value[..., -HALO:, :], axis, 1)
    below = from_behind(value[..., :HALO, :], axis, -1)
    return jnp.concatenate([above, value, below], axis=-2)


def gather_columns(value, axis):
    count = lax.axis_size(axis)
    copies = jnp.broadcast_to(value[None], (count,) + value.shape)
    pieces = lax.all_to_all(copies, axis, 0, 0, tiled=True)
    return pieces.transpose(1, 0, 2).reshape(value.shape[0], count * value.shape[1])


def scatter_sum_columns(value, axis):
    count = lax.axis_size(axis)
    rows, cols = value.shape
    pieces = value.reshape(rows, count, cols // count).transpose(1, 0, 2)
    return lax.all_to_all(pieces, axis, 0, 0, tiled=True).sum(axis=0)


def lane_shift(vector, shift):
    width = vector.shape[-1]
    pad = [(0, 0)] * (vector.ndim - 1) + [(abs(shift), abs(shift))]
    padded = jnp.pad(vector, pad)
    start = abs(shift) - shift
    return lax.slice_in_dim(padded, start, start + width, axis=vector.ndim - 1)


def shifted_in(value, axis, shift):
    config = [(0, 0, 0)] * value.ndim
    size = value.shape[axis]
    if shift > 0:
        config[axis] = (shift, 0, 0)
        kept = lax.slice_in_dim(value, 0, size - shift, axis=axis)
    else:
        config[axis] = (0, -shift, 0)
        kept = lax.slice_in_dim(value, -shift, size, axis=axis)
    return lax.pad(kept, jnp.zeros((), value.dtype), config)


def march_kernel(
    drive_ref, fwd_ref, adj_ref, src_above_ref, src_below_ref,
    dens_ref, dens_above_ref, dens_below_ref, matched_ref,
    final_ref, pieces_ref,
    source_ref, density_ref, step_ref, history_ref, sense_ref, gathered_ref,
):
    runs, waves, rows, cols = source_ref.shape
    own = fwd_ref.shape[1]
    reach = dens_above_ref.shape[0] - 1
    block_rows = pieces_ref.shape[1]
    for wave in range(waves):
        for run, own_ref in enumerate((fwd_ref, adj_ref)):
            source_ref[run, wave, 0:HALO] = src_above_ref[run, wave]
            source_ref[run, wave, HALO : HALO + own] = own_ref[wave]
            source_ref[run, wave, HALO + own : rows] = src_below_ref[run, wave]
    density_ref[...] = jnp.zeros((rows, cols), jnp.float32)
    density_ref[HALO - reach : HALO] = dens_above_ref[0:reach]
    density_ref[HALO : HALO + own] = dens_ref[...]
    density_ref[HALO + own : HALO + own + reach] = dens_below_ref[1 : reach + 1]
    step_ref[0:HALO] = jnp.broadcast_to(time_step * dens_above_ref[reach : reach + 1], (HALO, cols))
    step_ref[HALO : HALO + own] = jnp.full((own, cols), time_step, jnp.float32)
    step_ref[HALO + own : rows] = jnp.broadcast_to(time_step * dens_below_ref[0:1], (HALO, cols))
    row_id = lax.broadcasted_iota(jnp.int32, (rows, cols), 0)
    col_id = lax.broadcasted_iota(jnp.int32, (rows, cols), 1)
    density = density_ref[...]
    hy_step = step_ref[...]
    inverse = jnp.where(hy_step > 0.0, time_step / (1.0 + high_contrast * density), 0.0)
    sense_ref[...] = jnp.zeros((rows, cols), jnp.float32)
    for wave in range(waves):
        for run in range(runs):
            field_e = jnp.zeros((rows, cols), jnp.float32)
            field_hx = jnp.zeros((rows, cols), jnp.float32)
            field_hy = jnp.zeros((rows, cols), jnp.float32)
            current = jnp.zeros((rows, cols), jnp.float32)
            for turn in range(ITERS):
                e_up = jnp.where(row_id < rows - 1, pltpu.roll(field_e, rows - 1, 0), 0.0)
                e_right = jnp.where(col_id < cols - 1, pltpu.roll(field_e, cols - 1, 1), 0.0)
                field_hx = field_hx - time_step * (e_right - field_e)
                field_hy = field_hy + hy_step * (e_up - field_e)
                current = drude_decay * current + drude_gain * density * field_e
                hy_down = jnp.where(row_id > 0, pltpu.roll(field_hy, 1, 0), 0.0)
                hx_left = jnp.where(col_id > 0, pltpu.roll(field_hx, 1, 1), 0.0)
                field_e = (
                    field_e
                    + inverse * (field_hy - hy_down - (field_hx - hx_left) - current)
                    + drive_ref[turn, wave] * source_ref[run, wave]
                )
                if run == 0:
                    history_ref[turn] = field_e
                else:
                    sense_ref[...] += field_e * history_ref[ITERS - 1 - turn]
            if run == 0:
                final_ref[wave] = field_e
    scaled = GRAD_SCALE * sense_ref[HALO : HALO + own]
    lane = lax.broadcasted_iota(jnp.int32, (1, cols), 1)
    for row in range(block_rows):
        acc = jnp.zeros((1, cols), jnp.float32)
        for slot, shift in enumerate(SHIFTS):
            code = row * len(SHIFTS) + slot
            per_col = jnp.sum(matched_ref[code] * scaled, axis=0, keepdims=True)
            moved = FACTOR * shift
            inside = (lane >= moved) & (lane < cols + moved)
            acc = acc + jnp.where(inside, pltpu.roll(per_col, moved % cols, 1), 0.0)
        gathered_ref[row : row + 1] = acc
    gathered_ref[block_rows:] = jnp.zeros((gathered_ref.shape[0] - block_rows, cols), jnp.float32)
    span = pieces_ref.shape[2]
    width = span * FACTOR
    spread = (
        lax.broadcasted_iota(jnp.int32, (width, span), 0) // FACTOR
        == lax.broadcasted_iota(jnp.int32, (width, span), 1)
    ).astype(jnp.float32)
    for chunk in range(pieces_ref.shape[0]):
        pieces_ref[chunk] = jnp.dot(
            gathered_ref[:, chunk * width : (chunk + 1) * width], spread,
            precision=lax.Precision.HIGHEST, preferred_element_type=jnp.float32,
        )[:block_rows]


def march(drive, fwd, adj, src_above, src_below, dens, dens_above, dens_below, matched, block_rows, chunks):
    runs, waves, _, cols = src_above.shape
    rows = fwd.shape[1] + 2 * HALO
    vmem = pltpu.MemorySpace.VMEM
    smem = pltpu.MemorySpace.SMEM
    return pl.pallas_call(
        march_kernel,
        out_shape=(
            jax.ShapeDtypeStruct((waves, rows, cols), jnp.float32),
            jax.ShapeDtypeStruct((chunks, block_rows, 128), jnp.float32),
        ),
        in_specs=[pl.BlockSpec(memory_space=smem)] + [pl.BlockSpec(memory_space=vmem)] * 8,
        out_specs=(pl.BlockSpec(memory_space=vmem), pl.BlockSpec(memory_space=vmem)),
        scratch_shapes=[
            pltpu.VMEM((runs, waves, rows, cols), jnp.float32),
            pltpu.VMEM((rows, cols), jnp.float32),
            pltpu.VMEM((rows, cols), jnp.float32),
            pltpu.VMEM((ITERS, rows, cols), jnp.float32),
            pltpu.VMEM((rows, cols), jnp.float32),
            pltpu.VMEM((8, cols), jnp.float32),
        ],
    )(drive, fwd, adj, src_above, src_below, dens, dens_above, dens_below, matched)


def shards(density, foot_index, foot_weight, source_fwd, source_adj, omega):
    sources = jnp.stack([source_fwd, source_adj])
    src_above = from_behind(sources[:, :, -HALO:], "tile", 1)
    src_below = from_behind(sources[:, :, :HALO], "tile", -1)
    strip = gather_columns(density, "wl")
    block_rows, block_cols = strip.shape
    cells_x, cells_y = foot_index.shape[1:]
    factor = cells_y // block_cols
    assert factor == FACTOR and high_contrast / (source_fwd.shape[0] * lax.axis_size("wl")) == GRAD_SCALE
    weights = foot_weight.astype(jnp.float32)
    col_block = lax.broadcasted_iota(jnp.int32, (1, cells_y), 1) // factor
    key = (foot_index // block_cols) * len(SHIFTS) + (foot_index % block_cols - col_block[None]) + 2
    codes = lax.broadcasted_iota(jnp.int32, (block_rows * len(SHIFTS), 1, 1), 0)
    matched = jnp.zeros((block_rows * len(SHIFTS), cells_x, cells_y), jnp.float32)
    for entry in range(foot_index.shape[0]):
        matched = matched + jnp.where(key[entry][None] == codes, weights[entry][None], 0.0)
    drive = jnp.stack([jnp.sin(omega * (turn + 1.0)) for turn in range(ITERS)])
    matched, drive = lax.optimization_barrier((matched, drive))
    span = 128
    chunks = block_cols // span
    spread = (
        lax.broadcasted_iota(jnp.int32, (span, span * factor), 1) // factor
        == lax.broadcasted_iota(jnp.int32, (span, span * factor), 0)
    ).astype(jnp.float32)
    shifted = jnp.stack([lane_shift(strip[row], -shift) for row in range(block_rows) for shift in SHIFTS])
    candidates = jnp.dot(
        shifted.reshape(-1, span), spread, precision=lax.Precision.HIGHEST
    ).reshape(block_rows * len(SHIFTS), cells_y)
    reach = 2
    last_rows = jnp.sum(matched[:, -reach:] * candidates[:, None, :], axis=0)
    first_rows = jnp.sum(matched[:, :reach] * candidates[:, None, :], axis=0)
    present = jnp.ones((1, cells_y), jnp.float32)
    above = from_behind(jnp.concatenate([last_rows, present]), "tile", 1)
    below = from_behind(jnp.concatenate([present, first_rows]), "tile", -1)
    density_cell = jnp.sum(matched * candidates[:, None, :], axis=0)
    final, pieces = march(
        drive, source_fwd, source_adj, src_above, src_below, density_cell, above, below, matched, block_rows, chunks
    )
    count = lax.axis_size("wl")
    density_grad = lax.all_to_all(
        pieces.reshape(count, chunks // count, block_rows, span).transpose(0, 2, 1, 3).reshape(count, block_rows, -1),
        "wl", 0, 0, tiled=True,
    ).sum(axis=0)
    return (final[:, HALO : HALO + cells_x], density_grad)


def solution(mesh):
    in_specs = (
        P("tile", "wl"),
        P(None, "tile", None),
        P(None, "tile", None),
        P("wl", "tile", None),
        P("wl", "tile", None),
        P("wl"),
    )
    out_specs = (P("wl", "tile", None), P("tile", "wl"))
    return jax.shard_map(shards, mesh=mesh, in_specs=in_specs, out_specs=out_specs, check_vma=False)
```

```python
import jax
import jax.numpy as jnp
from jax import lax
from jax.experimental import pallas as pl
from jax.experimental.pallas import tpu as pltpu
from jax.sharding import PartitionSpec as P

ITERS = 4
HALO = 4
FACTOR = 4
GRAD_SCALE = 4.0 / 16
SHIFTS = (-2, -1, 0, 1, 2)


time_step = 0.5
high_contrast = 4.0
drude_decay = 0.9
drude_gain = 0.5


def from_behind(value, axis, steps):
    count = lax.axis_size(axis)
    first, last = (max(0, -steps), min(count, count - steps))
    return lax.ppermute(value, axis, [(source, source + steps) for source in range(first, last)])


def with_halo(value, axis):
    above = from_behind(value[..., -HALO:, :], axis, 1)
    below = from_behind(value[..., :HALO, :], axis, -1)
    return jnp.concatenate([above, value, below], axis=-2)


def gather_columns(value, axis):
    count = lax.axis_size(axis)
    copies = jnp.broadcast_to(value[None], (count,) + value.shape)
    pieces = lax.all_to_all(copies, axis, 0, 0, tiled=True)
    return pieces.transpose(1, 0, 2).reshape(value.shape[0], count * value.shape[1])


def scatter_sum_columns(value, axis):
    count = lax.axis_size(axis)
    rows, cols = value.shape
    pieces = value.reshape(rows, count, cols // count).transpose(1, 0, 2)
    return lax.all_to_all(pieces, axis, 0, 0, tiled=True).sum(axis=0)


def lane_shift(vector, shift):
    width = vector.shape[-1]
    pad = [(0, 0)] * (vector.ndim - 1) + [(abs(shift), abs(shift))]
    padded = jnp.pad(vector, pad)
    start = abs(shift) - shift
    return lax.slice_in_dim(padded, start, start + width, axis=vector.ndim - 1)


def shifted_in(value, axis, shift):
    config = [(0, 0, 0)] * value.ndim
    size = value.shape[axis]
    if shift > 0:
        config[axis] = (shift, 0, 0)
        kept = lax.slice_in_dim(value, 0, size - shift, axis=axis)
    else:
        config[axis] = (0, -shift, 0)
        kept = lax.slice_in_dim(value, -shift, size, axis=axis)
    return lax.pad(kept, jnp.zeros((), value.dtype), config)


def march_kernel(
    drive_ref, fwd_ref, adj_ref, src_above_hbm, src_below_hbm,
    dens_ref, dens_above_hbm, dens_below_hbm, matched_ref,
    final_ref, pieces_ref,
    source_ref, density_ref, step_ref, history_ref, sense_ref, gathered_ref,
    src_above_ref, src_below_ref, dens_above_ref, dens_below_ref, copy_sems,
):
    copies = [
        pltpu.make_async_copy(src_above_hbm, src_above_ref, copy_sems.at[0]),
        pltpu.make_async_copy(src_below_hbm, src_below_ref, copy_sems.at[1]),
        pltpu.make_async_copy(dens_above_hbm, dens_above_ref, copy_sems.at[2]),
        pltpu.make_async_copy(dens_below_hbm, dens_below_ref, copy_sems.at[3]),
    ]
    for copy in copies:
        copy.start()
    runs, waves, rows, cols = source_ref.shape
    own = fwd_ref.shape[1]
    reach = dens_above_ref.shape[0] - 1
    block_rows = pieces_ref.shape[1]
    copies[0].wait()
    copies[1].wait()
    for wave in range(waves):
        for run, own_ref in enumerate((fwd_ref, adj_ref)):
            source_ref[run, wave, 0:HALO] = src_above_ref[run, wave]
            source_ref[run, wave, HALO : HALO + own] = own_ref[wave]
            source_ref[run, wave, HALO + own : rows] = src_below_ref[run, wave]
    density_ref[...] = jnp.zeros((rows, cols), jnp.float32)
    copies[2].wait()
    copies[3].wait()
    density_ref[HALO - reach : HALO] = dens_above_ref[0:reach]
    density_ref[HALO : HALO + own] = dens_ref[...]
    density_ref[HALO + own : HALO + own + reach] = dens_below_ref[1 : reach + 1]
    step_ref[0:HALO] = jnp.broadcast_to(time_step * dens_above_ref[reach : reach + 1], (HALO, cols))
    step_ref[HALO : HALO + own] = jnp.full((own, cols), time_step, jnp.float32)
    step_ref[HALO + own : rows] = jnp.broadcast_to(time_step * dens_below_ref[0:1], (HALO, cols))
    row_id = lax.broadcasted_iota(jnp.int32, (rows, cols), 0)
    col_id = lax.broadcasted_iota(jnp.int32, (rows, cols), 1)
    density = density_ref[...]
    half_density = drude_gain * density
    hy_step = step_ref[...]
    inverse = jnp.where(hy_step > 0.0, time_step / (1.0 + high_contrast * density), 0.0)
    sense_ref[...] = jnp.zeros((rows, cols), jnp.float32)
    for wave in range(waves):
        for run in range(runs):
            field_e = jnp.zeros((rows, cols), jnp.float32)
            field_hx = jnp.zeros((rows, cols), jnp.float32)
            field_hy = jnp.zeros((rows, cols), jnp.float32)
            current = jnp.zeros((rows, cols), jnp.float32)
            for turn in range(ITERS):
                e_up = pltpu.roll(field_e, rows - 1, 0)
                e_right = jnp.where(col_id < cols - 1, pltpu.roll(field_e, cols - 1, 1), 0.0)
                field_hx = field_hx - time_step * (e_right - field_e)
                field_hy = field_hy + hy_step * (e_up - field_e)
                current = drude_decay * current + half_density * field_e
                hy_down = pltpu.roll(field_hy, 1, 0)
                hx_left = jnp.where(col_id > 0, pltpu.roll(field_hx, 1, 1), 0.0)
                field_e = (
                    field_e
                    + inverse * (field_hy - hy_down - (field_hx - hx_left) - current)
                    + drive_ref[turn, wave] * source_ref[run, wave]
                )
                if run == 0:
                    history_ref[turn] = field_e
                else:
                    sense_ref[...] += field_e * history_ref[ITERS - 1 - turn]
            if run == 0:
                final_ref[wave] = field_e
    scaled = GRAD_SCALE * sense_ref[HALO : HALO + own]
    lane = lax.broadcasted_iota(jnp.int32, (1, cols), 1)
    for row in range(block_rows):
        acc = jnp.zeros((1, cols), jnp.float32)
        for slot, shift in enumerate(SHIFTS):
            code = row * len(SHIFTS) + slot
            per_col = jnp.sum(matched_ref[code] * scaled, axis=0, keepdims=True)
            moved = FACTOR * shift
            inside = (lane >= moved) & (lane < cols + moved)
            acc = acc + jnp.where(inside, pltpu.roll(per_col, moved % cols, 1), 0.0)
        gathered_ref[row : row + 1] = acc
    gathered_ref[block_rows:] = jnp.zeros((gathered_ref.shape[0] - block_rows, cols), jnp.float32)
    span = pieces_ref.shape[2]
    width = span * FACTOR
    spread = (
        lax.broadcasted_iota(jnp.int32, (width, span), 0) // FACTOR
        == lax.broadcasted_iota(jnp.int32, (width, span), 1)
    ).astype(jnp.float32)
    for chunk in range(pieces_ref.shape[0]):
        pieces_ref[chunk] = jnp.dot(
            gathered_ref[:, chunk * width : (chunk + 1) * width], spread,
            precision=lax.Precision.HIGHEST, preferred_element_type=jnp.float32,
        )[:block_rows]


def march(drive, fwd, adj, src_above, src_below, dens, dens_above, dens_below, matched, block_rows, chunks):
    runs, waves, _, cols = src_above.shape
    rows = fwd.shape[1] + 2 * HALO
    vmem = pltpu.MemorySpace.VMEM
    smem = pltpu.MemorySpace.SMEM
    return pl.pallas_call(
        march_kernel,
        out_shape=(
            jax.ShapeDtypeStruct((waves, rows, cols), jnp.float32),
            jax.ShapeDtypeStruct((chunks, block_rows, 128), jnp.float32),
        ),
        in_specs=[pl.BlockSpec(memory_space=smem)]
        + [pl.BlockSpec(memory_space=vmem)] * 2
        + [pl.BlockSpec(memory_space=pl.ANY)] * 2
        + [pl.BlockSpec(memory_space=vmem)]
        + [pl.BlockSpec(memory_space=pl.ANY)] * 2
        + [pl.BlockSpec(memory_space=vmem)],
        out_specs=(pl.BlockSpec(memory_space=vmem), pl.BlockSpec(memory_space=vmem)),
        scratch_shapes=[
            pltpu.VMEM((runs, waves, rows, cols), jnp.float32),
            pltpu.VMEM((rows, cols), jnp.float32),
            pltpu.VMEM((rows, cols), jnp.float32),
            pltpu.VMEM((ITERS, rows, cols), jnp.float32),
            pltpu.VMEM((rows, cols), jnp.float32),
            pltpu.VMEM((8, cols), jnp.float32),
            pltpu.VMEM(src_above.shape, jnp.float32),
            pltpu.VMEM(src_below.shape, jnp.float32),
            pltpu.VMEM(dens_above.shape, jnp.float32),
            pltpu.VMEM(dens_below.shape, jnp.float32),
            pltpu.SemaphoreType.DMA((4,)),
        ],
    )(drive, fwd, adj, src_above, src_below, dens, dens_above, dens_below, matched)


def shards(density, foot_index, foot_weight, source_fwd, source_adj, omega):
    sources = jnp.stack([source_fwd, source_adj])
    src_above = from_behind(sources[:, :, -HALO:], "tile", 1)
    src_below = from_behind(sources[:, :, :HALO], "tile", -1)
    strip = gather_columns(density, "wl")
    block_rows, block_cols = strip.shape
    cells_x, cells_y = foot_index.shape[1:]
    factor = cells_y // block_cols
    assert factor == FACTOR and high_contrast / (source_fwd.shape[0] * lax.axis_size("wl")) == GRAD_SCALE
    weights = foot_weight.astype(jnp.float32)
    col_block = lax.broadcasted_iota(jnp.int32, (1, cells_y), 1) // factor
    key = (foot_index // block_cols) * len(SHIFTS) + (foot_index % block_cols - col_block[None]) + 2
    codes = lax.broadcasted_iota(jnp.int32, (block_rows * len(SHIFTS), 1, 1), 0)
    matched = jnp.zeros((block_rows * len(SHIFTS), cells_x, cells_y), jnp.float32)
    for entry in range(foot_index.shape[0]):
        matched = matched + jnp.where(key[entry][None] == codes, weights[entry][None], 0.0)
    drive = jnp.stack([jnp.sin(omega * (turn + 1.0)) for turn in range(ITERS)])
    matched, drive = lax.optimization_barrier((matched, drive))
    span = 128
    chunks = block_cols // span
    spread = (
        lax.broadcasted_iota(jnp.int32, (span, span * factor), 1) // factor
        == lax.broadcasted_iota(jnp.int32, (span, span * factor), 0)
    ).astype(jnp.float32)
    shifted = jnp.stack([lane_shift(strip[row], -shift) for row in range(block_rows) for shift in SHIFTS])
    candidates = jnp.dot(
        shifted.reshape(-1, span), spread, precision=lax.Precision.HIGHEST
    ).reshape(block_rows * len(SHIFTS), cells_y)
    reach = 2
    last_rows = jnp.sum(matched[:, -reach:] * candidates[:, None, :], axis=0)
    first_rows = jnp.sum(matched[:, :reach] * candidates[:, None, :], axis=0)
    present = jnp.ones((1, cells_y), jnp.float32)
    above = from_behind(jnp.concatenate([last_rows, present]), "tile", 1)
    below = from_behind(jnp.concatenate([present, first_rows]), "tile", -1)
    density_cell = jnp.sum(matched * candidates[:, None, :], axis=0)
    final, pieces = march(
        drive, source_fwd, source_adj, src_above, src_below, density_cell, above, below, matched, block_rows, chunks
    )
    count = lax.axis_size("wl")
    density_grad = lax.all_to_all(
        pieces.reshape(count, chunks // count, block_rows, span).transpose(0, 2, 1, 3).reshape(count, block_rows, -1),
        "wl", 0, 0, tiled=True,
    ).sum(axis=0)
    return (final[:, HALO : HALO + cells_x], density_grad)


def solution(mesh):
    in_specs = (
        P("tile", "wl"),
        P(None, "tile", None),
        P(None, "tile", None),
        P("wl", "tile", None),
        P("wl", "tile", None),
        P("wl"),
    )
    out_specs = (P("wl", "tile", None), P("tile", "wl"))
    return jax.shard_map(shards, mesh=mesh, in_specs=in_specs, out_specs=out_specs, check_vma=False)
```

```python
import jax
import jax.numpy as jnp
from jax import lax
from jax.experimental import pallas as pl
from jax.experimental.pallas import tpu as pltpu
from jax.sharding import PartitionSpec as P

ITERS = 4
HALO = 4
FACTOR = 4
GRAD_SCALE = 4.0 / 16
SHIFTS = (-2, -1, 0, 1, 2)


time_step = 0.5
high_contrast = 4.0
drude_decay = 0.9
drude_gain = 0.5


def from_behind(value, axis, steps):
    count = lax.axis_size(axis)
    first, last = (max(0, -steps), min(count, count - steps))
    return lax.ppermute(value, axis, [(source, source + steps) for source in range(first, last)])


def with_halo(value, axis):
    above = from_behind(value[..., -HALO:, :], axis, 1)
    below = from_behind(value[..., :HALO, :], axis, -1)
    return jnp.concatenate([above, value, below], axis=-2)


def gather_columns(value, axis):
    count = lax.axis_size(axis)
    copies = jnp.broadcast_to(value[None], (count,) + value.shape)
    pieces = lax.all_to_all(copies, axis, 0, 0, tiled=True)
    return pieces.transpose(1, 0, 2).reshape(value.shape[0], count * value.shape[1])


def scatter_sum_columns(value, axis):
    count = lax.axis_size(axis)
    rows, cols = value.shape
    pieces = value.reshape(rows, count, cols // count).transpose(1, 0, 2)
    return lax.all_to_all(pieces, axis, 0, 0, tiled=True).sum(axis=0)


def lane_shift(vector, shift):
    width = vector.shape[-1]
    pad = [(0, 0)] * (vector.ndim - 1) + [(abs(shift), abs(shift))]
    padded = jnp.pad(vector, pad)
    start = abs(shift) - shift
    return lax.slice_in_dim(padded, start, start + width, axis=vector.ndim - 1)


def shifted_in(value, axis, shift):
    config = [(0, 0, 0)] * value.ndim
    size = value.shape[axis]
    if shift > 0:
        config[axis] = (shift, 0, 0)
        kept = lax.slice_in_dim(value, 0, size - shift, axis=axis)
    else:
        config[axis] = (0, -shift, 0)
        kept = lax.slice_in_dim(value, -shift, size, axis=axis)
    return lax.pad(kept, jnp.zeros((), value.dtype), config)


def march_kernel(
    drive_ref, fwd_ref, adj_ref, src_above_ref, src_below_ref,
    dens_ref, dens_above_ref, dens_below_ref, matched_ref,
    final_ref, pieces_ref,
    source_ref, density_ref, step_ref, history_ref, sense_ref, gathered_ref,
):
    runs, waves, rows, cols = source_ref.shape
    own = fwd_ref.shape[1]
    reach = dens_above_ref.shape[0] - 1
    block_rows = pieces_ref.shape[1]
    for wave in range(waves):
        for run, own_ref in enumerate((fwd_ref, adj_ref)):
            source_ref[run, wave, 0:HALO] = src_above_ref[run, wave]
            source_ref[run, wave, HALO : HALO + own] = own_ref[wave]
            source_ref[run, wave, HALO + own : rows] = src_below_ref[run, wave]
    density_ref[...] = jnp.zeros((rows, cols), jnp.float32)
    density_ref[HALO - reach : HALO] = dens_above_ref[0:reach]
    density_ref[HALO : HALO + own] = dens_ref[...]
    density_ref[HALO + own : HALO + own + reach] = dens_below_ref[1 : reach + 1]
    step_ref[0:HALO] = jnp.broadcast_to(time_step * dens_above_ref[reach : reach + 1], (HALO, cols))
    step_ref[HALO : HALO + own] = jnp.full((own, cols), time_step, jnp.float32)
    step_ref[HALO + own : rows] = jnp.broadcast_to(time_step * dens_below_ref[0:1], (HALO, cols))
    row_id = lax.broadcasted_iota(jnp.int32, (rows, cols), 0)
    col_id = lax.broadcasted_iota(jnp.int32, (rows, cols), 1)
    density = density_ref[...]
    half_density = drude_gain * density
    hy_step = step_ref[...]
    inverse = jnp.where(hy_step > 0.0, time_step / (1.0 + high_contrast * density), 0.0)
    sense_ref[...] = jnp.zeros((rows, cols), jnp.float32)
    for wave in range(waves):
        for run in range(runs):
            field_e = jnp.zeros((rows, cols), jnp.float32)
            field_hx = jnp.zeros((rows, cols), jnp.float32)
            field_hy = jnp.zeros((rows, cols), jnp.float32)
            current = jnp.zeros((rows, cols), jnp.float32)
            for turn in range(ITERS):
                e_up = jnp.where(row_id < rows - 1, pltpu.roll(field_e, rows - 1, 0), 0.0)
                e_right = jnp.where(col_id < cols - 1, pltpu.roll(field_e, cols - 1, 1), 0.0)
                field_hx = field_hx - time_step * (e_right - field_e)
                field_hy = field_hy + hy_step * (e_up - field_e)
                current = drude_decay * current + half_density * field_e
                hy_down = jnp.where(row_id > 0, pltpu.roll(field_hy, 1, 0), 0.0)
                hx_left = jnp.where(col_id > 0, pltpu.roll(field_hx, 1, 1), 0.0)
                field_e = (
                    field_e
                    + inverse * (field_hy - hy_down - (field_hx - hx_left) - current)
                    + drive_ref[turn, wave] * source_ref[run, wave]
                )
                if run == 0:
                    history_ref[turn] = field_e
                else:
                    sense_ref[...] += field_e * history_ref[ITERS - 1 - turn]
            if run == 0:
                final_ref[wave] = field_e
    scaled = GRAD_SCALE * sense_ref[HALO : HALO + own]
    lane = lax.broadcasted_iota(jnp.int32, (1, cols), 1)
    for row in range(block_rows):
        acc = jnp.zeros((1, cols), jnp.float32)
        for slot, shift in enumerate(SHIFTS):
            code = row * len(SHIFTS) + slot
            per_col = jnp.sum(matched_ref[code] * scaled, axis=0, keepdims=True)
            moved = FACTOR * shift
            inside = (lane >= moved) & (lane < cols + moved)
            acc = acc + jnp.where(inside, pltpu.roll(per_col, moved % cols, 1), 0.0)
        gathered_ref[row : row + 1] = acc
    gathered_ref[block_rows:] = jnp.zeros((gathered_ref.shape[0] - block_rows, cols), jnp.float32)
    span = pieces_ref.shape[2]
    width = span * FACTOR
    spread = (
        lax.broadcasted_iota(jnp.int32, (width, span), 0) // FACTOR
        == lax.broadcasted_iota(jnp.int32, (width, span), 1)
    ).astype(jnp.float32)
    for chunk in range(pieces_ref.shape[0]):
        pieces_ref[chunk] = jnp.dot(
            gathered_ref[:, chunk * width : (chunk + 1) * width], spread,
            precision=lax.Precision.HIGHEST, preferred_element_type=jnp.float32,
        )[:block_rows]


def march(drive, fwd, adj, src_above, src_below, dens, dens_above, dens_below, matched, block_rows, chunks):
    runs, waves, _, cols = src_above.shape
    rows = fwd.shape[1] + 2 * HALO
    vmem = pltpu.MemorySpace.VMEM
    smem = pltpu.MemorySpace.SMEM
    return pl.pallas_call(
        march_kernel,
        out_shape=(
            jax.ShapeDtypeStruct((waves, rows, cols), jnp.float32),
            jax.ShapeDtypeStruct((chunks, block_rows, 128), jnp.float32),
        ),
        in_specs=[pl.BlockSpec(memory_space=smem)] + [pl.BlockSpec(memory_space=vmem)] * 8,
        out_specs=(pl.BlockSpec(memory_space=vmem), pl.BlockSpec(memory_space=vmem)),
        scratch_shapes=[
            pltpu.VMEM((runs, waves, rows, cols), jnp.float32),
            pltpu.VMEM((rows, cols), jnp.float32),
            pltpu.VMEM((rows, cols), jnp.float32),
            pltpu.VMEM((ITERS, rows, cols), jnp.float32),
            pltpu.VMEM((rows, cols), jnp.float32),
            pltpu.VMEM((8, cols), jnp.float32),
        ],
    )(drive, fwd, adj, src_above, src_below, dens, dens_above, dens_below, matched)


def shards(density, foot_index, foot_weight, source_fwd, source_adj, omega):
    sources = jnp.stack([source_fwd, source_adj])
    src_above = from_behind(sources[:, :, -HALO:], "tile", 1)
    src_below = from_behind(sources[:, :, :HALO], "tile", -1)
    strip = gather_columns(density, "wl")
    block_rows, block_cols = strip.shape
    cells_x, cells_y = foot_index.shape[1:]
    factor = cells_y // block_cols
    assert factor == FACTOR and high_contrast / (source_fwd.shape[0] * lax.axis_size("wl")) == GRAD_SCALE
    weights = foot_weight.astype(jnp.float32)
    col_block = lax.broadcasted_iota(jnp.int32, (1, cells_y), 1) // factor
    key = (foot_index // block_cols) * len(SHIFTS) + (foot_index % block_cols - col_block[None]) + 2
    codes = lax.broadcasted_iota(jnp.int32, (block_rows * len(SHIFTS), 1, 1), 0)
    matched = jnp.zeros((block_rows * len(SHIFTS), cells_x, cells_y), jnp.float32)
    for entry in range(foot_index.shape[0]):
        matched = matched + jnp.where(key[entry][None] == codes, weights[entry][None], 0.0)
    drive = jnp.stack([jnp.sin(omega * (turn + 1.0)) for turn in range(ITERS)])
    matched, drive = lax.optimization_barrier((matched, drive))
    span = 128
    chunks = block_cols // span
    spread = (
        lax.broadcasted_iota(jnp.int32, (span, span * factor), 1) // factor
        == lax.broadcasted_iota(jnp.int32, (span, span * factor), 0)
    ).astype(jnp.float32)
    shifted = jnp.stack([lane_shift(strip[row], -shift) for row in range(block_rows) for shift in SHIFTS])
    candidates = jnp.dot(
        shifted.reshape(-1, span), spread, precision=lax.Precision.HIGHEST
    ).reshape(block_rows * len(SHIFTS), cells_y)
    reach = 2
    last_rows = jnp.sum(matched[:, -reach:] * candidates[:, None, :], axis=0)
    first_rows = jnp.sum(matched[:, :reach] * candidates[:, None, :], axis=0)
    present = jnp.ones((1, cells_y), jnp.float32)
    above = from_behind(jnp.concatenate([last_rows, present]), "tile", 1)
    below = from_behind(jnp.concatenate([present, first_rows]), "tile", -1)
    density_cell = jnp.sum(matched * candidates[:, None, :], axis=0)
    final, pieces = march(
        drive, source_fwd, source_adj, src_above, src_below, density_cell, above, below, matched, block_rows, chunks
    )
    count = lax.axis_size("wl")
    density_grad = lax.all_to_all(
        pieces.reshape(count, chunks // count, block_rows, span).transpose(0, 2, 1, 3).reshape(count, block_rows, -1),
        "wl", 0, 0, tiled=True,
    ).sum(axis=0)
    return (final[:, HALO : HALO + cells_x], density_grad)


def solution(mesh):
    in_specs = (
        P("tile", "wl"),
        P(None, "tile", None),
        P(None, "tile", None),
        P("wl", "tile", None),
        P("wl", "tile", None),
        P("wl"),
    )
    out_specs = (P("wl", "tile", None), P("tile", "wl"))
    return jax.shard_map(shards, mesh=mesh, in_specs=in_specs, out_specs=out_specs, check_vma=False)
```

```python
import jax
import jax.numpy as jnp
from jax import lax
from jax.experimental import pallas as pl
from jax.experimental.pallas import tpu as pltpu
from jax.sharding import PartitionSpec as P

ITERS = 4
HALO = 4
FACTOR = 4
GRAD_SCALE = 4.0 / 16
SHIFTS = (-2, -1, 0, 1, 2)


time_step = 0.5
high_contrast = 4.0
drude_decay = 0.9
drude_gain = 0.5


def from_behind(value, axis, steps):
    count = lax.axis_size(axis)
    first, last = (max(0, -steps), min(count, count - steps))
    return lax.ppermute(value, axis, [(source, source + steps) for source in range(first, last)])


def with_halo(value, axis):
    above = from_behind(value[..., -HALO:, :], axis, 1)
    below = from_behind(value[..., :HALO, :], axis, -1)
    return jnp.concatenate([above, value, below], axis=-2)


def gather_columns(value, axis):
    count = lax.axis_size(axis)
    copies = jnp.broadcast_to(value[None], (count,) + value.shape)
    pieces = lax.all_to_all(copies, axis, 0, 0, tiled=True)
    return pieces.transpose(1, 0, 2).reshape(value.shape[0], count * value.shape[1])


def scatter_sum_columns(value, axis):
    count = lax.axis_size(axis)
    rows, cols = value.shape
    pieces = value.reshape(rows, count, cols // count).transpose(1, 0, 2)
    return lax.all_to_all(pieces, axis, 0, 0, tiled=True).sum(axis=0)


def lane_shift(vector, shift):
    width = vector.shape[-1]
    pad = [(0, 0)] * (vector.ndim - 1) + [(abs(shift), abs(shift))]
    padded = jnp.pad(vector, pad)
    start = abs(shift) - shift
    return lax.slice_in_dim(padded, start, start + width, axis=vector.ndim - 1)


def shifted_in(value, axis, shift):
    config = [(0, 0, 0)] * value.ndim
    size = value.shape[axis]
    if shift > 0:
        config[axis] = (shift, 0, 0)
        kept = lax.slice_in_dim(value, 0, size - shift, axis=axis)
    else:
        config[axis] = (0, -shift, 0)
        kept = lax.slice_in_dim(value, -shift, size, axis=axis)
    return lax.pad(kept, jnp.zeros((), value.dtype), config)


def march_kernel(
    drive_ref, fwd_ref, adj_ref, src_above_ref, src_below_ref,
    dens_ref, dens_above_ref, dens_below_ref, matched_ref,
    final_ref, pieces_ref,
    source_ref, density_ref, step_ref, history_ref, sense_ref, gathered_ref,
):
    runs, waves, rows, cols = source_ref.shape
    own = fwd_ref.shape[1]
    reach = dens_above_ref.shape[0] - 1
    block_rows = pieces_ref.shape[1]
    for wave in range(waves):
        for run, own_ref in enumerate((fwd_ref, adj_ref)):
            source_ref[run, wave, 0:HALO] = src_above_ref[run, wave]
            source_ref[run, wave, HALO : HALO + own] = own_ref[wave]
            source_ref[run, wave, HALO + own : rows] = src_below_ref[run, wave]
    density_ref[...] = jnp.zeros((rows, cols), jnp.float32)
    density_ref[HALO - reach : HALO] = dens_above_ref[0:reach]
    density_ref[HALO : HALO + own] = dens_ref[...]
    density_ref[HALO + own : HALO + own + reach] = dens_below_ref[1 : reach + 1]
    step_ref[0:HALO] = jnp.broadcast_to(time_step * dens_above_ref[reach : reach + 1], (HALO, cols))
    step_ref[HALO : HALO + own] = jnp.full((own, cols), time_step, jnp.float32)
    step_ref[HALO + own : rows] = jnp.broadcast_to(time_step * dens_below_ref[0:1], (HALO, cols))
    row_id = lax.broadcasted_iota(jnp.int32, (rows, cols), 0)
    col_id = lax.broadcasted_iota(jnp.int32, (rows, cols), 1)
    density = density_ref[...]
    half_density = drude_gain * density
    hy_step = step_ref[...]
    inverse = jnp.where(hy_step > 0.0, time_step / (1.0 + high_contrast * density), 0.0)
    sense_ref[...] = jnp.zeros((rows, cols), jnp.float32)
    for wave in range(waves):
        for run in range(runs):
            field_e = field_hx = field_hy = current = None
            for turn in range(ITERS):
                drive_term = drive_ref[turn, wave] * source_ref[run, wave]
                if field_e is None:
                    field_e = drive_term
                else:
                    e_up = jnp.where(row_id < rows - 1, pltpu.roll(field_e, rows - 1, 0), 0.0)
                    e_right = jnp.where(col_id < cols - 1, pltpu.roll(field_e, cols - 1, 1), 0.0)
                    if field_hx is None:
                        field_hx = -time_step * (e_right - field_e)
                        field_hy = hy_step * (e_up - field_e)
                        current = half_density * field_e
                    else:
                        field_hx = field_hx - time_step * (e_right - field_e)
                        field_hy = field_hy + hy_step * (e_up - field_e)
                        current = drude_decay * current + half_density * field_e
                    hy_down = jnp.where(row_id > 0, pltpu.roll(field_hy, 1, 0), 0.0)
                    hx_left = jnp.where(col_id > 0, pltpu.roll(field_hx, 1, 1), 0.0)
                    field_e = (
                        field_e
                        + inverse * (field_hy - hy_down - (field_hx - hx_left) - current)
                        + drive_term
                    )
                if run == 0:
                    history_ref[turn] = field_e
                else:
                    sense_ref[...] += field_e * history_ref[ITERS - 1 - turn]
            if run == 0:
                final_ref[wave] = field_e
    scaled = GRAD_SCALE * sense_ref[HALO : HALO + own]
    lane = lax.broadcasted_iota(jnp.int32, (1, cols), 1)
    for row in range(block_rows):
        acc = jnp.zeros((1, cols), jnp.float32)
        for slot, shift in enumerate(SHIFTS):
            code = row * len(SHIFTS) + slot
            per_col = jnp.sum(matched_ref[code] * scaled, axis=0, keepdims=True)
            moved = FACTOR * shift
            inside = (lane >= moved) & (lane < cols + moved)
            acc = acc + jnp.where(inside, pltpu.roll(per_col, moved % cols, 1), 0.0)
        gathered_ref[row : row + 1] = acc
    gathered_ref[block_rows:] = jnp.zeros((gathered_ref.shape[0] - block_rows, cols), jnp.float32)
    span = pieces_ref.shape[2]
    width = span * FACTOR
    spread = (
        lax.broadcasted_iota(jnp.int32, (width, span), 0) // FACTOR
        == lax.broadcasted_iota(jnp.int32, (width, span), 1)
    ).astype(jnp.float32)
    for chunk in range(pieces_ref.shape[0]):
        pieces_ref[chunk] = jnp.dot(
            gathered_ref[:, chunk * width : (chunk + 1) * width], spread,
            precision=lax.Precision.HIGHEST, preferred_element_type=jnp.float32,
        )[:block_rows]


def march(drive, fwd, adj, src_above, src_below, dens, dens_above, dens_below, matched, block_rows, chunks):
    runs, waves, _, cols = src_above.shape
    rows = fwd.shape[1] + 2 * HALO
    vmem = pltpu.MemorySpace.VMEM
    smem = pltpu.MemorySpace.SMEM
    return pl.pallas_call(
        march_kernel,
        out_shape=(
            jax.ShapeDtypeStruct((waves, rows, cols), jnp.float32),
            jax.ShapeDtypeStruct((chunks, block_rows, 128), jnp.float32),
        ),
        in_specs=[pl.BlockSpec(memory_space=smem)] + [pl.BlockSpec(memory_space=vmem)] * 8,
        out_specs=(pl.BlockSpec(memory_space=vmem), pl.BlockSpec(memory_space=vmem)),
        scratch_shapes=[
            pltpu.VMEM((runs, waves, rows, cols), jnp.float32),
            pltpu.VMEM((rows, cols), jnp.float32),
            pltpu.VMEM((rows, cols), jnp.float32),
            pltpu.VMEM((ITERS, rows, cols), jnp.float32),
            pltpu.VMEM((rows, cols), jnp.float32),
            pltpu.VMEM((8, cols), jnp.float32),
        ],
    )(drive, fwd, adj, src_above, src_below, dens, dens_above, dens_below, matched)


def shards(density, foot_index, foot_weight, source_fwd, source_adj, omega):
    sources = jnp.stack([source_fwd, source_adj])
    src_above = from_behind(sources[:, :, -HALO:], "tile", 1)
    src_below = from_behind(sources[:, :, :HALO], "tile", -1)
    strip = gather_columns(density, "wl")
    block_rows, block_cols = strip.shape
    cells_x, cells_y = foot_index.shape[1:]
    factor = cells_y // block_cols
    assert factor == FACTOR and high_contrast / (source_fwd.shape[0] * lax.axis_size("wl")) == GRAD_SCALE
    weights = foot_weight.astype(jnp.float32)
    col_block = lax.broadcasted_iota(jnp.int32, (1, cells_y), 1) // factor
    key = (foot_index // block_cols) * len(SHIFTS) + (foot_index % block_cols - col_block[None]) + 2
    codes = lax.broadcasted_iota(jnp.int32, (block_rows * len(SHIFTS), 1, 1), 0)
    matched = jnp.zeros((block_rows * len(SHIFTS), cells_x, cells_y), jnp.float32)
    for entry in range(foot_index.shape[0]):
        matched = matched + jnp.where(key[entry][None] == codes, weights[entry][None], 0.0)
    drive = jnp.stack([jnp.sin(omega * (turn + 1.0)) for turn in range(ITERS)])
    matched, drive = lax.optimization_barrier((matched, drive))
    span = 128
    chunks = block_cols // span
    spread = (
        lax.broadcasted_iota(jnp.int32, (span, span * factor), 1) // factor
        == lax.broadcasted_iota(jnp.int32, (span, span * factor), 0)
    ).astype(jnp.float32)
    shifted = jnp.stack([lane_shift(strip[row], -shift) for row in range(block_rows) for shift in SHIFTS])
    candidates = jnp.dot(
        shifted.reshape(-1, span), spread, precision=lax.Precision.HIGHEST
    ).reshape(block_rows * len(SHIFTS), cells_y)
    reach = 2
    last_rows = jnp.sum(matched[:, -reach:] * candidates[:, None, :], axis=0)
    first_rows = jnp.sum(matched[:, :reach] * candidates[:, None, :], axis=0)
    present = jnp.ones((1, cells_y), jnp.float32)
    above = from_behind(jnp.concatenate([last_rows, present]), "tile", 1)
    below = from_behind(jnp.concatenate([present, first_rows]), "tile", -1)
    density_cell = jnp.sum(matched * candidates[:, None, :], axis=0)
    final, pieces = march(
        drive, source_fwd, source_adj, src_above, src_below, density_cell, above, below, matched, block_rows, chunks
    )
    count = lax.axis_size("wl")
    density_grad = lax.all_to_all(
        pieces.reshape(count, chunks // count, block_rows, span).transpose(0, 2, 1, 3).reshape(count, block_rows, -1),
        "wl", 0, 0, tiled=True,
    ).sum(axis=0)
    return (final[:, HALO : HALO + cells_x], density_grad)


def solution(mesh):
    in_specs = (
        P("tile", "wl"),
        P(None, "tile", None),
        P(None, "tile", None),
        P("wl", "tile", None),
        P("wl", "tile", None),
        P("wl"),
    )
    out_specs = (P("wl", "tile", None), P("tile", "wl"))
    return jax.shard_map(shards, mesh=mesh, in_specs=in_specs, out_specs=out_specs, check_vma=False)
```

```python
import jax
import jax.numpy as jnp
from jax import lax
from jax.experimental import pallas as pl
from jax.experimental.pallas import tpu as pltpu
from jax.sharding import PartitionSpec as P

ITERS = 4
HALO = 4
FACTOR = 4
CHUNK = 512
GRAD_SCALE = 4.0 / 16
SHIFTS = (-2, -1, 0, 1, 2)


time_step = 0.5
high_contrast = 4.0
drude_decay = 0.9
drude_gain = 0.5


def from_behind(value, axis, steps):
    count = lax.axis_size(axis)
    first, last = (max(0, -steps), min(count, count - steps))
    return lax.ppermute(value, axis, [(source, source + steps) for source in range(first, last)])


def with_halo(value, axis):
    above = from_behind(value[..., -HALO:, :], axis, 1)
    below = from_behind(value[..., :HALO, :], axis, -1)
    return jnp.concatenate([above, value, below], axis=-2)


def gather_columns(value, axis):
    count = lax.axis_size(axis)
    copies = jnp.broadcast_to(value[None], (count,) + value.shape)
    pieces = lax.all_to_all(copies, axis, 0, 0, tiled=True)
    return pieces.transpose(1, 0, 2).reshape(value.shape[0], count * value.shape[1])


def scatter_sum_columns(value, axis):
    count = lax.axis_size(axis)
    rows, cols = value.shape
    pieces = value.reshape(rows, count, cols // count).transpose(1, 0, 2)
    return lax.all_to_all(pieces, axis, 0, 0, tiled=True).sum(axis=0)


def lane_shift(vector, shift):
    width = vector.shape[-1]
    pad = [(0, 0)] * (vector.ndim - 1) + [(abs(shift), abs(shift))]
    padded = jnp.pad(vector, pad)
    start = abs(shift) - shift
    return lax.slice_in_dim(padded, start, start + width, axis=vector.ndim - 1)


def shifted_in(value, axis, shift):
    config = [(0, 0, 0)] * value.ndim
    size = value.shape[axis]
    if shift > 0:
        config[axis] = (shift, 0, 0)
        kept = lax.slice_in_dim(value, 0, size - shift, axis=axis)
    else:
        config[axis] = (0, -shift, 0)
        kept = lax.slice_in_dim(value, -shift, size, axis=axis)
    return lax.pad(kept, jnp.zeros((), value.dtype), config)


def march_kernel(
    drive_ref, fwd_ref, adj_ref, src_above_ref, src_below_ref,
    dens_ref, dens_above_ref, dens_below_ref, matched_ref,
    final_ref, pieces_ref,
    source_ref, density_ref, step_ref, history_ref, sense_ref, gathered_ref, fields_ref,
):
    runs, waves, rows, cols = source_ref.shape
    own = fwd_ref.shape[1]
    reach = dens_above_ref.shape[0] - 1
    block_rows = pieces_ref.shape[1]
    for wave in range(waves):
        for run, own_ref in enumerate((fwd_ref, adj_ref)):
            source_ref[run, wave, 0:HALO] = src_above_ref[run, wave]
            source_ref[run, wave, HALO : HALO + own] = own_ref[wave]
            source_ref[run, wave, HALO + own : rows] = src_below_ref[run, wave]
    density_ref[...] = jnp.zeros((rows, cols), jnp.float32)
    density_ref[HALO - reach : HALO] = dens_above_ref[0:reach]
    density_ref[HALO : HALO + own] = dens_ref[...]
    density_ref[HALO + own : HALO + own + reach] = dens_below_ref[1 : reach + 1]
    step_ref[0:HALO] = jnp.broadcast_to(time_step * dens_above_ref[reach : reach + 1], (HALO, cols))
    step_ref[HALO : HALO + own] = jnp.full((own, cols), time_step, jnp.float32)
    step_ref[HALO + own : rows] = jnp.broadcast_to(time_step * dens_below_ref[0:1], (HALO, cols))
    density = density_ref[...]
    fields_ref[4] = jnp.where(step_ref[...] > 0.0, time_step / (1.0 + high_contrast * density), 0.0)
    fields_ref[5] = drude_gain * density
    sense_ref[...] = jnp.zeros((rows, cols), jnp.float32)
    width = CHUNK
    count = cols // width
    row_id = lax.broadcasted_iota(jnp.int32, (rows, width), 0)
    for wave in range(waves):
        for run in range(runs):
            field_e = drive_ref[0, wave] * source_ref[run, wave]
            fields_ref[0] = field_e
            if run == 0:
                history_ref[0] = field_e
            else:
                sense_ref[...] += field_e * history_ref[ITERS - 1]
            for turn in range(1, ITERS):

                def sweep(index, carry, turn=turn, run=run, wave=wave):
                    at = pl.multiple_of(index * width, width)
                    ahead = pl.multiple_of(jnp.minimum(index + 1, count - 1) * width, width)
                    here = pl.ds(at, width)
                    field_e = fields_ref[0, :, here]
                    e_next = jnp.where(index + 1 < count, fields_ref[0, :, pl.ds(ahead, 128)], 0.0)
                    e_right = pltpu.roll(jnp.concatenate([field_e, e_next], axis=1), width + 127, 1)[:, :width]
                    e_up = jnp.where(row_id < rows - 1, pltpu.roll(field_e, rows - 1, 0), 0.0)
                    hy_step = step_ref[:, here]
                    half_density = fields_ref[5, :, here]
                    if turn == 1:
                        field_hx = -time_step * (e_right - field_e)
                        field_hy = hy_step * (e_up - field_e)
                        current = half_density * field_e
                    else:
                        field_hx = fields_ref[1, :, here] - time_step * (e_right - field_e)
                        field_hy = fields_ref[2, :, here] + hy_step * (e_up - field_e)
                        current = drude_decay * fields_ref[3, :, here] + half_density * field_e
                    hx_left = pltpu.roll(jnp.concatenate([carry, field_hx], axis=1), 1, 1)[:, 128:]
                    hy_down = jnp.where(row_id > 0, pltpu.roll(field_hy, 1, 0), 0.0)
                    field_e = (
                        field_e
                        + fields_ref[4, :, here] * (field_hy - hy_down - (field_hx - hx_left) - current)
                        + drive_ref[turn, wave] * source_ref[run, wave, :, here]
                    )
                    fields_ref[0, :, here] = field_e
                    fields_ref[1, :, here] = field_hx
                    fields_ref[2, :, here] = field_hy
                    fields_ref[3, :, here] = current
                    if run == 0:
                        history_ref[turn, :, here] = field_e
                    else:
                        sense_ref[:, here] += field_e * history_ref[ITERS - 1 - turn, :, here]
                    return field_hx[:, width - 128 :]

                lax.fori_loop(0, count, sweep, jnp.zeros((rows, 128), jnp.float32))
            if run == 0:
                final_ref[wave] = fields_ref[0]
    scaled = GRAD_SCALE * sense_ref[HALO : HALO + own]
    lane = lax.broadcasted_iota(jnp.int32, (1, cols), 1)
    for row in range(block_rows):
        acc = jnp.zeros((1, cols), jnp.float32)
        for slot, shift in enumerate(SHIFTS):
            code = row * len(SHIFTS) + slot
            per_col = jnp.sum(matched_ref[code] * scaled, axis=0, keepdims=True)
            moved = FACTOR * shift
            inside = (lane >= moved) & (lane < cols + moved)
            acc = acc + jnp.where(inside, pltpu.roll(per_col, moved % cols, 1), 0.0)
        gathered_ref[row : row + 1] = acc
    gathered_ref[block_rows:] = jnp.zeros((gathered_ref.shape[0] - block_rows, cols), jnp.float32)
    span = pieces_ref.shape[2]
    width = span * FACTOR
    spread = (
        lax.broadcasted_iota(jnp.int32, (width, span), 0) // FACTOR
        == lax.broadcasted_iota(jnp.int32, (width, span), 1)
    ).astype(jnp.float32)
    for chunk in range(pieces_ref.shape[0]):
        pieces_ref[chunk] = jnp.dot(
            gathered_ref[:, chunk * width : (chunk + 1) * width], spread,
            precision=lax.Precision.HIGHEST, preferred_element_type=jnp.float32,
        )[:block_rows]


def march(drive, fwd, adj, src_above, src_below, dens, dens_above, dens_below, matched, block_rows, chunks):
    runs, waves, _, cols = src_above.shape
    rows = fwd.shape[1] + 2 * HALO
    vmem = pltpu.MemorySpace.VMEM
    smem = pltpu.MemorySpace.SMEM
    return pl.pallas_call(
        march_kernel,
        out_shape=(
            jax.ShapeDtypeStruct((waves, rows, cols), jnp.float32),
            jax.ShapeDtypeStruct((chunks, block_rows, 128), jnp.float32),
        ),
        in_specs=[pl.BlockSpec(memory_space=smem)] + [pl.BlockSpec(memory_space=vmem)] * 8,
        out_specs=(pl.BlockSpec(memory_space=vmem), pl.BlockSpec(memory_space=vmem)),
        scratch_shapes=[
            pltpu.VMEM((runs, waves, rows, cols), jnp.float32),
            pltpu.VMEM((rows, cols), jnp.float32),
            pltpu.VMEM((rows, cols), jnp.float32),
            pltpu.VMEM((ITERS, rows, cols), jnp.float32),
            pltpu.VMEM((rows, cols), jnp.float32),
            pltpu.VMEM((8, cols), jnp.float32),
            pltpu.VMEM((6, rows, cols), jnp.float32),
        ],
    )(drive, fwd, adj, src_above, src_below, dens, dens_above, dens_below, matched)


def shards(density, foot_index, foot_weight, source_fwd, source_adj, omega):
    sources = jnp.stack([source_fwd, source_adj])
    src_above = from_behind(sources[:, :, -HALO:], "tile", 1)
    src_below = from_behind(sources[:, :, :HALO], "tile", -1)
    strip = gather_columns(density, "wl")
    block_rows, block_cols = strip.shape
    cells_x, cells_y = foot_index.shape[1:]
    factor = cells_y // block_cols
    assert factor == FACTOR and high_contrast / (source_fwd.shape[0] * lax.axis_size("wl")) == GRAD_SCALE
    weights = foot_weight.astype(jnp.float32)
    col_block = lax.broadcasted_iota(jnp.int32, (1, cells_y), 1) // factor
    key = (foot_index // block_cols) * len(SHIFTS) + (foot_index % block_cols - col_block[None]) + 2
    codes = lax.broadcasted_iota(jnp.int32, (block_rows * len(SHIFTS), 1, 1), 0)
    matched = jnp.zeros((block_rows * len(SHIFTS), cells_x, cells_y), jnp.float32)
    for entry in range(foot_index.shape[0]):
        matched = matched + jnp.where(key[entry][None] == codes, weights[entry][None], 0.0)
    drive = jnp.stack([jnp.sin(omega * (turn + 1.0)) for turn in range(ITERS)])
    matched, drive = lax.optimization_barrier((matched, drive))
    span = 128
    chunks = block_cols // span
    spread = (
        lax.broadcasted_iota(jnp.int32, (span, span * factor), 1) // factor
        == lax.broadcasted_iota(jnp.int32, (span, span * factor), 0)
    ).astype(jnp.float32)
    shifted = jnp.stack([lane_shift(strip[row], -shift) for row in range(block_rows) for shift in SHIFTS])
    candidates = jnp.dot(
        shifted.reshape(-1, span), spread, precision=lax.Precision.HIGHEST
    ).reshape(block_rows * len(SHIFTS), cells_y)
    reach = 2
    last_rows = jnp.sum(matched[:, -reach:] * candidates[:, None, :], axis=0)
    first_rows = jnp.sum(matched[:, :reach] * candidates[:, None, :], axis=0)
    present = jnp.ones((1, cells_y), jnp.float32)
    above = from_behind(jnp.concatenate([last_rows, present]), "tile", 1)
    below = from_behind(jnp.concatenate([present, first_rows]), "tile", -1)
    density_cell = jnp.sum(matched * candidates[:, None, :], axis=0)
    final, pieces = march(
        drive, source_fwd, source_adj, src_above, src_below, density_cell, above, below, matched, block_rows, chunks
    )
    count = lax.axis_size("wl")
    density_grad = lax.all_to_all(
        pieces.reshape(count, chunks // count, block_rows, span).transpose(0, 2, 1, 3).reshape(count, block_rows, -1),
        "wl", 0, 0, tiled=True,
    ).sum(axis=0)
    return (final[:, HALO : HALO + cells_x], density_grad)


def solution(mesh):
    in_specs = (
        P("tile", "wl"),
        P(None, "tile", None),
        P(None, "tile", None),
        P("wl", "tile", None),
        P("wl", "tile", None),
        P("wl"),
    )
    out_specs = (P("wl", "tile", None), P("tile", "wl"))
    return jax.shard_map(shards, mesh=mesh, in_specs=in_specs, out_specs=out_specs, check_vma=False)
```

```python
import jax
import jax.numpy as jnp
import numpy as np
from jax import lax
from jax.experimental import pallas as pl
from jax.experimental.pallas import tpu as pltpu
from jax.sharding import PartitionSpec as P

ITERS = 4
HALO = 4
FACTOR = 4
GRAD_SCALE = 4.0 / 16
SHIFTS = (-2, -1, 0, 1, 2)


time_step = 0.5
high_contrast = 4.0
drude_decay = 0.9
drude_gain = 0.5


def from_behind(value, axis, steps):
    count = lax.axis_size(axis)
    first, last = (max(0, -steps), min(count, count - steps))
    return lax.ppermute(value, axis, [(source, source + steps) for source in range(first, last)])


def with_halo(value, axis):
    above = from_behind(value[..., -HALO:, :], axis, 1)
    below = from_behind(value[..., :HALO, :], axis, -1)
    return jnp.concatenate([above, value, below], axis=-2)


def gather_columns(value, axis):
    count = lax.axis_size(axis)
    copies = jnp.broadcast_to(value[None], (count,) + value.shape)
    pieces = lax.all_to_all(copies, axis, 0, 0, tiled=True)
    return pieces.transpose(1, 0, 2).reshape(value.shape[0], count * value.shape[1])


def scatter_sum_columns(value, axis):
    count = lax.axis_size(axis)
    rows, cols = value.shape
    pieces = value.reshape(rows, count, cols // count).transpose(1, 0, 2)
    return lax.all_to_all(pieces, axis, 0, 0, tiled=True).sum(axis=0)


def lane_shift(vector, shift):
    width = vector.shape[-1]
    pad = [(0, 0)] * (vector.ndim - 1) + [(abs(shift), abs(shift))]
    padded = jnp.pad(vector, pad)
    start = abs(shift) - shift
    return lax.slice_in_dim(padded, start, start + width, axis=vector.ndim - 1)


def shifted_in(value, axis, shift):
    config = [(0, 0, 0)] * value.ndim
    size = value.shape[axis]
    if shift > 0:
        config[axis] = (shift, 0, 0)
        kept = lax.slice_in_dim(value, 0, size - shift, axis=axis)
    else:
        config[axis] = (0, -shift, 0)
        kept = lax.slice_in_dim(value, -shift, size, axis=axis)
    return lax.pad(kept, jnp.zeros((), value.dtype), config)


def march_kernel(
    drive_ref, fwd_ref, adj_ref, src_above_ref, src_below_ref,
    dens_ref, dens_above_ref, dens_below_ref, matched_ref,
    final_ref, pieces_ref,
    source_ref, density_ref, step_ref, history_ref, sense_ref, gathered_ref,
):
    runs, waves, rows, cols = source_ref.shape
    own = fwd_ref.shape[1]
    reach = dens_above_ref.shape[0] - 1
    block_rows = pieces_ref.shape[1]
    for wave in range(waves):
        for run, own_ref in enumerate((fwd_ref, adj_ref)):
            source_ref[run, wave, 0:HALO] = src_above_ref[run, wave]
            source_ref[run, wave, HALO : HALO + own] = own_ref[wave]
            source_ref[run, wave, HALO + own : rows] = src_below_ref[run, wave]
    density_ref[...] = jnp.zeros((rows, cols), jnp.float32)
    density_ref[HALO - reach : HALO] = dens_above_ref[0:reach]
    density_ref[HALO : HALO + own] = dens_ref[...]
    density_ref[HALO + own : HALO + own + reach] = dens_below_ref[1 : reach + 1]
    step_ref[0:HALO] = jnp.broadcast_to(time_step * dens_above_ref[reach : reach + 1], (HALO, cols))
    step_ref[HALO : HALO + own] = jnp.full((own, cols), time_step, jnp.float32)
    step_ref[HALO + own : rows] = jnp.broadcast_to(time_step * dens_below_ref[0:1], (HALO, cols))
    row_id = lax.broadcasted_iota(jnp.int32, (rows, cols), 0)
    col_id = lax.broadcasted_iota(jnp.int32, (rows, cols), 1)
    density = density_ref[...]
    half_density = drude_gain * density
    hy_step = step_ref[...]
    inverse = jnp.where(hy_step > 0.0, time_step / (1.0 + high_contrast * density), 0.0)
    sense_ref[...] = jnp.zeros((rows, cols), jnp.float32)
    for wave in range(waves):
        for run in range(runs):
            field_e = field_hx = field_hy = current = None
            for turn in range(ITERS):
                drive_term = drive_ref[turn, wave] * source_ref[run, wave]
                if field_e is None:
                    field_e = drive_term
                else:
                    e_up = jnp.where(row_id < rows - 1, pltpu.roll(field_e, rows - 1, 0), 0.0)
                    e_right = jnp.where(col_id < cols - 1, pltpu.roll(field_e, cols - 1, 1), 0.0)
                    if field_hx is None:
                        field_hx = -time_step * (e_right - field_e)
                        field_hy = hy_step * (e_up - field_e)
                        current = half_density * field_e
                    else:
                        field_hx = field_hx - time_step * (e_right - field_e)
                        field_hy = field_hy + hy_step * (e_up - field_e)
                        current = drude_decay * current + half_density * field_e
                    hy_down = jnp.where(row_id > 0, pltpu.roll(field_hy, 1, 0), 0.0)
                    hx_left = jnp.where(col_id > 0, pltpu.roll(field_hx, 1, 1), 0.0)
                    field_e = (
                        field_e
                        + inverse * (field_hy - hy_down - (field_hx - hx_left) - current)
                        + drive_term
                    )
                if run == 0:
                    history_ref[turn] = field_e
                else:
                    sense_ref[...] += field_e * history_ref[ITERS - 1 - turn]
            if run == 0:
                final_ref[wave] = field_e
    scaled = GRAD_SCALE * sense_ref[HALO : HALO + own]
    lane = lax.broadcasted_iota(jnp.int32, (1, cols), 1)
    for row in range(block_rows):
        acc = jnp.zeros((1, cols), jnp.float32)
        for slot, shift in enumerate(SHIFTS):
            code = row * len(SHIFTS) + slot
            per_col = jnp.sum(matched_ref[code] * scaled, axis=0, keepdims=True)
            moved = FACTOR * shift
            inside = (lane >= moved) & (lane < cols + moved)
            acc = acc + jnp.where(inside, pltpu.roll(per_col, moved % cols, 1), 0.0)
        gathered_ref[row : row + 1] = acc
    gathered_ref[block_rows:] = jnp.zeros((gathered_ref.shape[0] - block_rows, cols), jnp.float32)
    span = pieces_ref.shape[2]
    width = span * FACTOR
    spread = (
        lax.broadcasted_iota(jnp.int32, (width, span), 0) // FACTOR
        == lax.broadcasted_iota(jnp.int32, (width, span), 1)
    ).astype(jnp.float32)
    for chunk in range(pieces_ref.shape[0]):
        pieces_ref[chunk] = jnp.dot(
            gathered_ref[:, chunk * width : (chunk + 1) * width], spread,
            precision=lax.Precision.HIGHEST, preferred_element_type=jnp.float32,
        )[:block_rows]


def march(drive, fwd, adj, src_above, src_below, dens, dens_above, dens_below, matched, block_rows, chunks):
    runs, waves, _, cols = src_above.shape
    rows = fwd.shape[1] + 2 * HALO
    vmem = pltpu.MemorySpace.VMEM
    smem = pltpu.MemorySpace.SMEM
    return pl.pallas_call(
        march_kernel,
        out_shape=(
            jax.ShapeDtypeStruct((waves, rows, cols), jnp.float32),
            jax.ShapeDtypeStruct((chunks, block_rows, 128), jnp.float32),
        ),
        in_specs=[pl.BlockSpec(memory_space=smem)] + [pl.BlockSpec(memory_space=vmem)] * 8,
        out_specs=(pl.BlockSpec(memory_space=vmem), pl.BlockSpec(memory_space=vmem)),
        scratch_shapes=[
            pltpu.VMEM((runs, waves, rows, cols), jnp.float32),
            pltpu.VMEM((rows, cols), jnp.float32),
            pltpu.VMEM((rows, cols), jnp.float32),
            pltpu.VMEM((ITERS, rows, cols), jnp.float32),
            pltpu.VMEM((rows, cols), jnp.float32),
            pltpu.VMEM((8, cols), jnp.float32),
        ],
    )(drive, fwd, adj, src_above, src_below, dens, dens_above, dens_below, matched)


def shards(density, foot_index, foot_weight, source_fwd, source_adj, omega):
    sources = jnp.stack([source_fwd, source_adj])
    src_above = from_behind(sources[:, :, -HALO:], "tile", 1)
    src_below = from_behind(sources[:, :, :HALO], "tile", -1)
    strip = gather_columns(density, "wl")
    block_rows, block_cols = strip.shape
    cells_x, cells_y = foot_index.shape[1:]
    factor = cells_y // block_cols
    assert factor == FACTOR and high_contrast / (source_fwd.shape[0] * lax.axis_size("wl")) == GRAD_SCALE
    weights = foot_weight.astype(jnp.float32)
    col_block = lax.broadcasted_iota(jnp.int32, (1, cells_y), 1) // factor
    key = (foot_index // block_cols) * len(SHIFTS) + (foot_index % block_cols - col_block[None]) + 2
    codes = lax.broadcasted_iota(jnp.int32, (block_rows * len(SHIFTS), 1, 1), 0)
    matched = jnp.zeros((block_rows * len(SHIFTS), cells_x, cells_y), jnp.float32)
    for entry in range(foot_index.shape[0]):
        matched = matched + jnp.where(key[entry][None] == codes, weights[entry][None], 0.0)
    matched = lax.optimization_barrier(matched)
    span = 128
    chunks = block_cols // span
    spread = (
        lax.broadcasted_iota(jnp.int32, (span, span * factor), 1) // factor
        == lax.broadcasted_iota(jnp.int32, (span, span * factor), 0)
    ).astype(jnp.float32)
    shifted = jnp.stack([lane_shift(strip[row], -shift) for row in range(block_rows) for shift in SHIFTS])
    candidates = jnp.dot(
        shifted.reshape(-1, span), spread, precision=lax.Precision.HIGHEST
    ).reshape(block_rows * len(SHIFTS), cells_y)
    reach = 2
    last_rows = jnp.sum(matched[:, -reach:] * candidates[:, None, :], axis=0)
    first_rows = jnp.sum(matched[:, :reach] * candidates[:, None, :], axis=0)
    present = jnp.ones((1, cells_y), jnp.float32)
    above = from_behind(jnp.concatenate([last_rows, present]), "tile", 1)
    below = from_behind(jnp.concatenate([present, first_rows]), "tile", -1)
    density_cell = jnp.sum(matched * candidates[:, None, :], axis=0)
    drive = jnp.sin(omega[None, :] * np.arange(1.0, ITERS + 1.0, dtype=np.float32)[:, None])
    final, pieces = march(
        drive, source_fwd, source_adj, src_above, src_below, density_cell, above, below, matched, block_rows, chunks
    )
    count = lax.axis_size("wl")
    density_grad = lax.all_to_all(
        pieces.reshape(count, chunks // count, block_rows, span).transpose(0, 2, 1, 3).reshape(count, block_rows, -1),
        "wl", 0, 0, tiled=True,
    ).sum(axis=0)
    return (final[:, HALO : HALO + cells_x], density_grad)


def solution(mesh):
    in_specs = (
        P("tile", "wl"),
        P(None, "tile", None),
        P(None, "tile", None),
        P("wl", "tile", None),
        P("wl", "tile", None),
        P("wl"),
    )
    out_specs = (P("wl", "tile", None), P("tile", "wl"))
    return jax.shard_map(shards, mesh=mesh, in_specs=in_specs, out_specs=out_specs, check_vma=False)
```

```python
import jax
import jax.numpy as jnp
from jax import lax
from jax.experimental import pallas as pl
from jax.experimental.pallas import tpu as pltpu
from jax.sharding import PartitionSpec as P

ITERS = 4
HALO = 4
FACTOR = 4
GRAD_SCALE = 4.0 / 16
SHIFTS = (-2, -1, 0, 1, 2)


time_step = 0.5
high_contrast = 4.0
drude_decay = 0.9
drude_gain = 0.5


def from_behind(value, axis, steps):
    count = lax.axis_size(axis)
    first, last = (max(0, -steps), min(count, count - steps))
    return lax.ppermute(value, axis, [(source, source + steps) for source in range(first, last)])


def with_halo(value, axis):
    above = from_behind(value[..., -HALO:, :], axis, 1)
    below = from_behind(value[..., :HALO, :], axis, -1)
    return jnp.concatenate([above, value, below], axis=-2)


def gather_columns(value, axis):
    count = lax.axis_size(axis)
    copies = jnp.broadcast_to(value[None], (count,) + value.shape)
    pieces = lax.all_to_all(copies, axis, 0, 0, tiled=True)
    return pieces.transpose(1, 0, 2).reshape(value.shape[0], count * value.shape[1])


def scatter_sum_columns(value, axis):
    count = lax.axis_size(axis)
    rows, cols = value.shape
    pieces = value.reshape(rows, count, cols // count).transpose(1, 0, 2)
    return lax.all_to_all(pieces, axis, 0, 0, tiled=True).sum(axis=0)


def lane_shift(vector, shift):
    width = vector.shape[-1]
    pad = [(0, 0)] * (vector.ndim - 1) + [(abs(shift), abs(shift))]
    padded = jnp.pad(vector, pad)
    start = abs(shift) - shift
    return lax.slice_in_dim(padded, start, start + width, axis=vector.ndim - 1)


def shifted_in(value, axis, shift):
    config = [(0, 0, 0)] * value.ndim
    size = value.shape[axis]
    if shift > 0:
        config[axis] = (shift, 0, 0)
        kept = lax.slice_in_dim(value, 0, size - shift, axis=axis)
    else:
        config[axis] = (0, -shift, 0)
        kept = lax.slice_in_dim(value, -shift, size, axis=axis)
    return lax.pad(kept, jnp.zeros((), value.dtype), config)


def march_kernel(
    drive_ref, fwd_ref, adj_ref, src_above_ref, src_below_ref,
    dens_ref, dens_above_ref, dens_below_ref, matched_ref,
    final_ref, pieces_ref,
    source_ref, density_ref, step_ref, history_ref, sense_ref, gathered_ref,
):
    runs, waves, rows, cols = source_ref.shape
    own = fwd_ref.shape[1]
    reach = dens_above_ref.shape[0] - 1
    block_rows = pieces_ref.shape[1]
    for wave in range(waves):
        for run, own_ref in enumerate((fwd_ref, adj_ref)):
            source_ref[run, wave, 0:HALO] = src_above_ref[run, wave]
            source_ref[run, wave, HALO : HALO + own] = own_ref[wave]
            source_ref[run, wave, HALO + own : rows] = src_below_ref[run, wave]
    density_ref[...] = jnp.zeros((rows, cols), jnp.float32)
    density_ref[HALO - reach : HALO] = dens_above_ref[0:reach]
    density_ref[HALO : HALO + own] = dens_ref[...]
    density_ref[HALO + own : HALO + own + reach] = dens_below_ref[1 : reach + 1]
    step_ref[0:HALO] = jnp.broadcast_to(time_step * dens_above_ref[reach : reach + 1], (HALO, cols))
    step_ref[HALO : HALO + own] = jnp.full((own, cols), time_step, jnp.float32)
    step_ref[HALO + own : rows] = jnp.broadcast_to(time_step * dens_below_ref[0:1], (HALO, cols))
    row_id = lax.broadcasted_iota(jnp.int32, (rows, cols), 0)
    col_id = lax.broadcasted_iota(jnp.int32, (rows, cols), 1)
    density = density_ref[...]
    half_density = drude_gain * density
    hy_step = step_ref[...]
    inverse = jnp.where(hy_step > 0.0, time_step / (1.0 + high_contrast * density), 0.0)
    sense_ref[...] = jnp.zeros((rows, cols), jnp.float32)
    drives = [
        [
            jnp.concatenate(
                [jnp.sin(jnp.full((rows, 128), drive_ref[wave] * (turn + 1.0), jnp.float32))] * (cols // 128), axis=1
            )
            for wave in range(waves)
        ]
        for turn in range(ITERS)
    ]
    for wave in range(waves):
        for run in range(runs):
            field_e = field_hx = field_hy = current = None
            for turn in range(ITERS):
                drive_term = drives[turn][wave] * source_ref[run, wave]
                if field_e is None:
                    field_e = drive_term
                else:
                    e_up = jnp.where(row_id < rows - 1, pltpu.roll(field_e, rows - 1, 0), 0.0)
                    e_right = jnp.where(col_id < cols - 1, pltpu.roll(field_e, cols - 1, 1), 0.0)
                    if field_hx is None:
                        field_hx = -time_step * (e_right - field_e)
                        field_hy = hy_step * (e_up - field_e)
                        current = half_density * field_e
                    else:
                        field_hx = field_hx - time_step * (e_right - field_e)
                        field_hy = field_hy + hy_step * (e_up - field_e)
                        current = drude_decay * current + half_density * field_e
                    hy_down = jnp.where(row_id > 0, pltpu.roll(field_hy, 1, 0), 0.0)
                    hx_left = jnp.where(col_id > 0, pltpu.roll(field_hx, 1, 1), 0.0)
                    field_e = (
                        field_e
                        + inverse * (field_hy - hy_down - (field_hx - hx_left) - current)
                        + drive_term
                    )
                if run == 0:
                    history_ref[turn] = field_e
                else:
                    sense_ref[...] += field_e * history_ref[ITERS - 1 - turn]
            if run == 0:
                final_ref[wave] = field_e
    scaled = GRAD_SCALE * sense_ref[HALO : HALO + own]
    lane = lax.broadcasted_iota(jnp.int32, (1, cols), 1)
    for row in range(block_rows):
        acc = jnp.zeros((1, cols), jnp.float32)
        for slot, shift in enumerate(SHIFTS):
            code = row * len(SHIFTS) + slot
            per_col = jnp.sum(matched_ref[code] * scaled, axis=0, keepdims=True)
            moved = FACTOR * shift
            inside = (lane >= moved) & (lane < cols + moved)
            acc = acc + jnp.where(inside, pltpu.roll(per_col, moved % cols, 1), 0.0)
        gathered_ref[row : row + 1] = acc
    gathered_ref[block_rows:] = jnp.zeros((gathered_ref.shape[0] - block_rows, cols), jnp.float32)
    span = pieces_ref.shape[2]
    width = span * FACTOR
    spread = (
        lax.broadcasted_iota(jnp.int32, (width, span), 0) // FACTOR
        == lax.broadcasted_iota(jnp.int32, (width, span), 1)
    ).astype(jnp.float32)
    for chunk in range(pieces_ref.shape[0]):
        pieces_ref[chunk] = jnp.dot(
            gathered_ref[:, chunk * width : (chunk + 1) * width], spread,
            precision=lax.Precision.HIGHEST, preferred_element_type=jnp.float32,
        )[:block_rows]


def march(drive, fwd, adj, src_above, src_below, dens, dens_above, dens_below, matched, block_rows, chunks):
    runs, waves, _, cols = src_above.shape
    rows = fwd.shape[1] + 2 * HALO
    vmem = pltpu.MemorySpace.VMEM
    smem = pltpu.MemorySpace.SMEM
    return pl.pallas_call(
        march_kernel,
        out_shape=(
            jax.ShapeDtypeStruct((waves, rows, cols), jnp.float32),
            jax.ShapeDtypeStruct((chunks, block_rows, 128), jnp.float32),
        ),
        in_specs=[pl.BlockSpec(memory_space=smem)] + [pl.BlockSpec(memory_space=vmem)] * 8,
        out_specs=(pl.BlockSpec(memory_space=vmem), pl.BlockSpec(memory_space=vmem)),
        scratch_shapes=[
            pltpu.VMEM((runs, waves, rows, cols), jnp.float32),
            pltpu.VMEM((rows, cols), jnp.float32),
            pltpu.VMEM((rows, cols), jnp.float32),
            pltpu.VMEM((ITERS, rows, cols), jnp.float32),
            pltpu.VMEM((rows, cols), jnp.float32),
            pltpu.VMEM((8, cols), jnp.float32),
        ],
    )(drive, fwd, adj, src_above, src_below, dens, dens_above, dens_below, matched)


def shards(density, foot_index, foot_weight, source_fwd, source_adj, omega):
    sources = jnp.stack([source_fwd, source_adj])
    src_above = from_behind(sources[:, :, -HALO:], "tile", 1)
    src_below = from_behind(sources[:, :, :HALO], "tile", -1)
    strip = gather_columns(density, "wl")
    block_rows, block_cols = strip.shape
    cells_x, cells_y = foot_index.shape[1:]
    factor = cells_y // block_cols
    assert factor == FACTOR and high_contrast / (source_fwd.shape[0] * lax.axis_size("wl")) == GRAD_SCALE
    weights = foot_weight.astype(jnp.float32)
    col_block = lax.broadcasted_iota(jnp.int32, (1, cells_y), 1) // factor
    key = (foot_index // block_cols) * len(SHIFTS) + (foot_index % block_cols - col_block[None]) + 2
    codes = lax.broadcasted_iota(jnp.int32, (block_rows * len(SHIFTS), 1, 1), 0)
    matched = jnp.zeros((block_rows * len(SHIFTS), cells_x, cells_y), jnp.float32)
    for entry in range(foot_index.shape[0]):
        matched = matched + jnp.where(key[entry][None] == codes, weights[entry][None], 0.0)
    matched = lax.optimization_barrier(matched)
    span = 128
    chunks = block_cols // span
    spread = (
        lax.broadcasted_iota(jnp.int32, (span, span * factor), 1) // factor
        == lax.broadcasted_iota(jnp.int32, (span, span * factor), 0)
    ).astype(jnp.float32)
    shifted = jnp.stack([lane_shift(strip[row], -shift) for row in range(block_rows) for shift in SHIFTS])
    candidates = jnp.dot(
        shifted.reshape(-1, span), spread, precision=lax.Precision.HIGHEST
    ).reshape(block_rows * len(SHIFTS), cells_y)
    reach = 2
    last_rows = jnp.sum(matched[:, -reach:] * candidates[:, None, :], axis=0)
    first_rows = jnp.sum(matched[:, :reach] * candidates[:, None, :], axis=0)
    present = jnp.ones((1, cells_y), jnp.float32)
    above = from_behind(jnp.concatenate([last_rows, present]), "tile", 1)
    below = from_behind(jnp.concatenate([present, first_rows]), "tile", -1)
    density_cell = jnp.sum(matched * candidates[:, None, :], axis=0)
    final, pieces = march(
        omega, source_fwd, source_adj, src_above, src_below, density_cell, above, below, matched, block_rows, chunks
    )
    count = lax.axis_size("wl")
    density_grad = lax.all_to_all(
        pieces.reshape(count, chunks // count, block_rows, span).transpose(0, 2, 1, 3).reshape(count, block_rows, -1),
        "wl", 0, 0, tiled=True,
    ).sum(axis=0)
    return (final[:, HALO : HALO + cells_x], density_grad)


def solution(mesh):
    in_specs = (
        P("tile", "wl"),
        P(None, "tile", None),
        P(None, "tile", None),
        P("wl", "tile", None),
        P("wl", "tile", None),
        P("wl"),
    )
    out_specs = (P("wl", "tile", None), P("tile", "wl"))
    return jax.shard_map(shards, mesh=mesh, in_specs=in_specs, out_specs=out_specs, check_vma=False)
```

```python
import jax
import jax.numpy as jnp
from jax import lax
from jax.experimental import pallas as pl
from jax.experimental.pallas import tpu as pltpu
from jax.sharding import PartitionSpec as P

ITERS = 4
HALO = 4
FACTOR = 4
GRAD_SCALE = 4.0 / 16
SHIFTS = (-2, -1, 0, 1, 2)


time_step = 0.5
high_contrast = 4.0
drude_decay = 0.9
drude_gain = 0.5


def from_behind(value, axis, steps):
    count = lax.axis_size(axis)
    first, last = (max(0, -steps), min(count, count - steps))
    return lax.ppermute(value, axis, [(source, source + steps) for source in range(first, last)])


def with_halo(value, axis):
    above = from_behind(value[..., -HALO:, :], axis, 1)
    below = from_behind(value[..., :HALO, :], axis, -1)
    return jnp.concatenate([above, value, below], axis=-2)


def gather_columns(value, axis):
    count = lax.axis_size(axis)
    copies = jnp.broadcast_to(value[None], (count,) + value.shape)
    pieces = lax.all_to_all(copies, axis, 0, 0, tiled=True)
    return pieces.transpose(1, 0, 2).reshape(value.shape[0], count * value.shape[1])


def scatter_sum_columns(value, axis):
    count = lax.axis_size(axis)
    rows, cols = value.shape
    pieces = value.reshape(rows, count, cols // count).transpose(1, 0, 2)
    return lax.all_to_all(pieces, axis, 0, 0, tiled=True).sum(axis=0)


def lane_shift(vector, shift):
    width = vector.shape[-1]
    pad = [(0, 0)] * (vector.ndim - 1) + [(abs(shift), abs(shift))]
    padded = jnp.pad(vector, pad)
    start = abs(shift) - shift
    return lax.slice_in_dim(padded, start, start + width, axis=vector.ndim - 1)


def shifted_in(value, axis, shift):
    config = [(0, 0, 0)] * value.ndim
    size = value.shape[axis]
    if shift > 0:
        config[axis] = (shift, 0, 0)
        kept = lax.slice_in_dim(value, 0, size - shift, axis=axis)
    else:
        config[axis] = (0, -shift, 0)
        kept = lax.slice_in_dim(value, -shift, size, axis=axis)
    return lax.pad(kept, jnp.zeros((), value.dtype), config)


def march_kernel(
    drive_ref, fwd_ref, adj_ref, src_above_ref, src_below_ref,
    dens_ref, dens_above_ref, dens_below_ref, matched_ref,
    final_ref, pieces_ref,
    source_ref, density_ref, step_ref, history_ref, sense_ref, gathered_ref,
):
    runs, waves, rows, cols = source_ref.shape
    own = fwd_ref.shape[1]
    reach = dens_above_ref.shape[0] - 1
    block_rows = pieces_ref.shape[1]
    for wave in range(waves):
        for run, own_ref in enumerate((fwd_ref, adj_ref)):
            source_ref[run, wave, 0:HALO] = src_above_ref[run, wave]
            source_ref[run, wave, HALO : HALO + own] = own_ref[wave]
            source_ref[run, wave, HALO + own : rows] = src_below_ref[run, wave]
    density_ref[...] = jnp.zeros((rows, cols), jnp.float32)
    density_ref[HALO - reach : HALO] = dens_above_ref[0:reach]
    density_ref[HALO : HALO + own] = dens_ref[...]
    density_ref[HALO + own : HALO + own + reach] = dens_below_ref[1 : reach + 1]
    step_ref[0:HALO] = jnp.broadcast_to(time_step * dens_above_ref[reach : reach + 1], (HALO, cols))
    step_ref[HALO : HALO + own] = jnp.full((own, cols), time_step, jnp.float32)
    step_ref[HALO + own : rows] = jnp.broadcast_to(time_step * dens_below_ref[0:1], (HALO, cols))
    row_id = lax.broadcasted_iota(jnp.int32, (rows, cols), 0)
    col_id = lax.broadcasted_iota(jnp.int32, (rows, cols), 1)
    density = density_ref[...]
    half_density = drude_gain * density
    hy_step = step_ref[...]
    inverse = jnp.where(hy_step > 0.0, time_step / (1.0 + high_contrast * density), 0.0)
    sense_ref[...] = jnp.zeros((rows, cols), jnp.float32)
    drives = [
        [
            jnp.concatenate(
                [jnp.sin(jnp.full((rows, 128), drive_ref[wave] * (turn + 1.0), jnp.float32))] * (cols // 128), axis=1
            )
            for wave in range(waves)
        ]
        for turn in range(ITERS)
    ]
    for wave in range(waves):
        for run in range(runs):
            field_e = field_hx = field_hy = current = None
            for turn in range(ITERS):
                drive_term = drives[turn][wave] * source_ref[run, wave]
                if field_e is None:
                    field_e = drive_term
                else:
                    e_up = jnp.where(row_id < rows - 1, pltpu.roll(field_e, rows - 1, 0), 0.0)
                    e_right = jnp.where(col_id < cols - 1, pltpu.roll(field_e, cols - 1, 1), 0.0)
                    if field_hx is None:
                        field_hx = -time_step * (e_right - field_e)
                        field_hy = hy_step * (e_up - field_e)
                        current = half_density * field_e
                    else:
                        field_hx = field_hx - time_step * (e_right - field_e)
                        field_hy = field_hy + hy_step * (e_up - field_e)
                        current = drude_decay * current + half_density * field_e
                    hy_down = jnp.where(row_id > 0, pltpu.roll(field_hy, 1, 0), 0.0)
                    hx_left = jnp.where(col_id > 0, pltpu.roll(field_hx, 1, 1), 0.0)
                    field_e = (
                        field_e
                        + inverse * (field_hy - hy_down - (field_hx - hx_left) - current)
                        + drive_term
                    )
                if run == 0:
                    history_ref[turn] = field_e
                else:
                    sense_ref[...] += field_e * history_ref[ITERS - 1 - turn]
            if run == 0:
                final_ref[wave] = history_ref[ITERS - 1, HALO : HALO + own]
    scaled = GRAD_SCALE * sense_ref[HALO : HALO + own]
    lane = lax.broadcasted_iota(jnp.int32, (1, cols), 1)
    for row in range(block_rows):
        acc = jnp.zeros((1, cols), jnp.float32)
        for slot, shift in enumerate(SHIFTS):
            code = row * len(SHIFTS) + slot
            per_col = jnp.sum(matched_ref[code] * scaled, axis=0, keepdims=True)
            moved = FACTOR * shift
            inside = (lane >= moved) & (lane < cols + moved)
            acc = acc + jnp.where(inside, pltpu.roll(per_col, moved % cols, 1), 0.0)
        gathered_ref[row : row + 1] = acc
    gathered_ref[block_rows:] = jnp.zeros((gathered_ref.shape[0] - block_rows, cols), jnp.float32)
    span = pieces_ref.shape[2]
    width = span * FACTOR
    spread = (
        lax.broadcasted_iota(jnp.int32, (width, span), 0) // FACTOR
        == lax.broadcasted_iota(jnp.int32, (width, span), 1)
    ).astype(jnp.float32)
    for chunk in range(pieces_ref.shape[0]):
        pieces_ref[chunk] = jnp.dot(
            gathered_ref[:, chunk * width : (chunk + 1) * width], spread,
            precision=lax.Precision.HIGHEST, preferred_element_type=jnp.float32,
        )[:block_rows]


def march(drive, fwd, adj, src_above, src_below, dens, dens_above, dens_below, matched, block_rows, chunks):
    runs, waves, _, cols = src_above.shape
    rows = fwd.shape[1] + 2 * HALO
    vmem = pltpu.MemorySpace.VMEM
    smem = pltpu.MemorySpace.SMEM
    return pl.pallas_call(
        march_kernel,
        out_shape=(
            jax.ShapeDtypeStruct((waves, fwd.shape[1], cols), jnp.float32),
            jax.ShapeDtypeStruct((chunks, block_rows, 128), jnp.float32),
        ),
        in_specs=[pl.BlockSpec(memory_space=smem)] + [pl.BlockSpec(memory_space=vmem)] * 8,
        out_specs=(pl.BlockSpec(memory_space=vmem), pl.BlockSpec(memory_space=vmem)),
        scratch_shapes=[
            pltpu.VMEM((runs, waves, rows, cols), jnp.float32),
            pltpu.VMEM((rows, cols), jnp.float32),
            pltpu.VMEM((rows, cols), jnp.float32),
            pltpu.VMEM((ITERS, rows, cols), jnp.float32),
            pltpu.VMEM((rows, cols), jnp.float32),
            pltpu.VMEM((8, cols), jnp.float32),
        ],
    )(drive, fwd, adj, src_above, src_below, dens, dens_above, dens_below, matched)


def shards(density, foot_index, foot_weight, source_fwd, source_adj, omega):
    sources = jnp.stack([source_fwd, source_adj])
    src_above = from_behind(sources[:, :, -HALO:], "tile", 1)
    src_below = from_behind(sources[:, :, :HALO], "tile", -1)
    strip = gather_columns(density, "wl")
    block_rows, block_cols = strip.shape
    cells_x, cells_y = foot_index.shape[1:]
    factor = cells_y // block_cols
    assert factor == FACTOR and high_contrast / (source_fwd.shape[0] * lax.axis_size("wl")) == GRAD_SCALE
    weights = foot_weight.astype(jnp.float32)
    col_block = lax.broadcasted_iota(jnp.int32, (1, cells_y), 1) // factor
    key = (foot_index // block_cols) * len(SHIFTS) + (foot_index % block_cols - col_block[None]) + 2
    codes = lax.broadcasted_iota(jnp.int32, (block_rows * len(SHIFTS), 1, 1), 0)
    matched = jnp.zeros((block_rows * len(SHIFTS), cells_x, cells_y), jnp.float32)
    for entry in range(foot_index.shape[0]):
        matched = matched + jnp.where(key[entry][None] == codes, weights[entry][None], 0.0)
    span = 128
    chunks = block_cols // span
    spread = (
        lax.broadcasted_iota(jnp.int32, (span, span * factor), 1) // factor
        == lax.broadcasted_iota(jnp.int32, (span, span * factor), 0)
    ).astype(jnp.float32)
    shifted = jnp.stack([lane_shift(strip[row], -shift) for row in range(block_rows) for shift in SHIFTS])
    candidates = jnp.dot(
        shifted.reshape(-1, span), spread, precision=lax.Precision.HIGHEST
    ).reshape(block_rows * len(SHIFTS), cells_y)
    reach = 2
    last_rows = jnp.sum(matched[:, -reach:] * candidates[:, None, :], axis=0)
    first_rows = jnp.sum(matched[:, :reach] * candidates[:, None, :], axis=0)
    present = jnp.ones((1, cells_y), jnp.float32)
    above = from_behind(jnp.concatenate([last_rows, present]), "tile", 1)
    below = from_behind(jnp.concatenate([present, first_rows]), "tile", -1)
    density_cell = jnp.sum(matched * candidates[:, None, :], axis=0)
    final, pieces = march(
        omega, source_fwd, source_adj, src_above, src_below, density_cell, above, below, matched, block_rows, chunks
    )
    count = lax.axis_size("wl")
    density_grad = lax.all_to_all(
        pieces.reshape(count, chunks // count, block_rows, span).transpose(0, 2, 1, 3).reshape(count, block_rows, -1),
        "wl", 0, 0, tiled=True,
    ).sum(axis=0)
    return (final, density_grad)


def solution(mesh):
    in_specs = (
        P("tile", "wl"),
        P(None, "tile", None),
        P(None, "tile", None),
        P("wl", "tile", None),
        P("wl", "tile", None),
        P("wl"),
    )
    out_specs = (P("wl", "tile", None), P("tile", "wl"))
    return jax.shard_map(shards, mesh=mesh, in_specs=in_specs, out_specs=out_specs, check_vma=False)
```

```python
import jax
import jax.numpy as jnp
from jax import lax
from jax.experimental import pallas as pl
from jax.experimental.pallas import tpu as pltpu
from jax.sharding import PartitionSpec as P

ITERS = 4
HALO = 4
FACTOR = 4
GRAD_SCALE = 4.0 / 16
SHIFTS = (-2, -1, 0, 1, 2)


time_step = 0.5
high_contrast = 4.0
drude_decay = 0.9
drude_gain = 0.5


def from_behind(value, axis, steps):
    count = lax.axis_size(axis)
    first, last = (max(0, -steps), min(count, count - steps))
    return lax.ppermute(value, axis, [(source, source + steps) for source in range(first, last)])


def with_halo(value, axis):
    above = from_behind(value[..., -HALO:, :], axis, 1)
    below = from_behind(value[..., :HALO, :], axis, -1)
    return jnp.concatenate([above, value, below], axis=-2)


def gather_columns(value, axis):
    count = lax.axis_size(axis)
    copies = jnp.broadcast_to(value[None], (count,) + value.shape)
    pieces = lax.all_to_all(copies, axis, 0, 0, tiled=True)
    return pieces.transpose(1, 0, 2).reshape(value.shape[0], count * value.shape[1])


def scatter_sum_columns(value, axis):
    count = lax.axis_size(axis)
    rows, cols = value.shape
    pieces = value.reshape(rows, count, cols // count).transpose(1, 0, 2)
    return lax.all_to_all(pieces, axis, 0, 0, tiled=True).sum(axis=0)


def lane_shift(vector, shift):
    width = vector.shape[-1]
    pad = [(0, 0)] * (vector.ndim - 1) + [(abs(shift), abs(shift))]
    padded = jnp.pad(vector, pad)
    start = abs(shift) - shift
    return lax.slice_in_dim(padded, start, start + width, axis=vector.ndim - 1)


def shifted_in(value, axis, shift):
    config = [(0, 0, 0)] * value.ndim
    size = value.shape[axis]
    if shift > 0:
        config[axis] = (shift, 0, 0)
        kept = lax.slice_in_dim(value, 0, size - shift, axis=axis)
    else:
        config[axis] = (0, -shift, 0)
        kept = lax.slice_in_dim(value, -shift, size, axis=axis)
    return lax.pad(kept, jnp.zeros((), value.dtype), config)


def march_kernel(
    drive_ref, fwd_ref, adj_ref, src_above_ref, src_below_ref,
    dens_ref, dens_above_ref, dens_below_ref, matched_ref,
    final_ref, pieces_ref,
    source_ref, density_ref, step_ref, history_ref, sense_ref, gathered_ref,
):
    runs, waves, rows, cols = source_ref.shape
    own = fwd_ref.shape[1]
    reach = dens_above_ref.shape[0] - 1
    block_rows = pieces_ref.shape[1]
    for wave in range(waves):
        for run, own_ref in enumerate((fwd_ref, adj_ref)):
            source_ref[run, wave, 0:HALO] = src_above_ref[run, wave]
            source_ref[run, wave, HALO : HALO + own] = own_ref[wave]
            source_ref[run, wave, HALO + own : rows] = src_below_ref[run, wave]
    density_ref[...] = jnp.zeros((rows, cols), jnp.float32)
    density_ref[HALO - reach : HALO] = dens_above_ref[0:reach]
    density_ref[HALO : HALO + own] = dens_ref[...]
    density_ref[HALO + own : HALO + own + reach] = dens_below_ref[1 : reach + 1]
    step_ref[0:HALO] = jnp.broadcast_to(time_step * dens_above_ref[reach : reach + 1], (HALO, cols))
    step_ref[HALO : HALO + own] = jnp.full((own, cols), time_step, jnp.float32)
    step_ref[HALO + own : rows] = jnp.broadcast_to(time_step * dens_below_ref[0:1], (HALO, cols))
    row_id = lax.broadcasted_iota(jnp.int32, (rows, cols), 0)
    col_id = lax.broadcasted_iota(jnp.int32, (rows, cols), 1)
    density = density_ref[...]
    half_density = drude_gain * density
    hy_step = step_ref[...]
    inverse = jnp.where(hy_step > 0.0, time_step / (1.0 + high_contrast * density), 0.0)
    sense_ref[...] = jnp.zeros((rows, cols), jnp.float32)
    drives = [
        [
            jnp.concatenate(
                [jnp.sin(jnp.full((rows, 128), drive_ref[wave] * (turn + 1.0), jnp.float32))] * (cols // 128), axis=1
            )
            for wave in range(waves)
        ]
        for turn in range(ITERS)
    ]
    for wave in range(waves):
        for run in range(runs):
            field_e = field_hx = field_hy = current = None
            for turn in range(ITERS):
                drive_term = drives[turn][wave] * source_ref[run, wave]
                if field_e is None:
                    field_e = drive_term
                else:
                    e_up = jnp.where(row_id < rows - 1, pltpu.roll(field_e, rows - 1, 0), 0.0)
                    e_right = jnp.where(col_id < cols - 1, pltpu.roll(field_e, cols - 1, 1), 0.0)
                    if field_hx is None:
                        field_hx = -time_step * (e_right - field_e)
                        field_hy = hy_step * (e_up - field_e)
                        current = half_density * field_e
                    else:
                        field_hx = field_hx - time_step * (e_right - field_e)
                        field_hy = field_hy + hy_step * (e_up - field_e)
                        current = drude_decay * current + half_density * field_e
                    hy_down = jnp.where(row_id > 0, pltpu.roll(field_hy, 1, 0), 0.0)
                    hx_left = jnp.where(col_id > 0, pltpu.roll(field_hx, 1, 1), 0.0)
                    field_e = (
                        field_e
                        + inverse * (field_hy - hy_down - (field_hx - hx_left) - current)
                        + drive_term
                    )
                if run == 0:
                    history_ref[turn] = field_e
                else:
                    sense_ref[...] += field_e * history_ref[ITERS - 1 - turn]
            if run == 0:
                final_ref[wave] = history_ref[ITERS - 1, HALO : HALO + own]
    scaled = GRAD_SCALE * sense_ref[HALO : HALO + own]
    lane = lax.broadcasted_iota(jnp.int32, (1, cols), 1)
    for row in range(block_rows):
        acc = jnp.zeros((1, cols), jnp.float32)
        for slot, shift in enumerate(SHIFTS):
            code = row * len(SHIFTS) + slot
            per_col = jnp.sum(matched_ref[code] * scaled, axis=0, keepdims=True)
            moved = FACTOR * shift
            inside = (lane >= moved) & (lane < cols + moved)
            acc = acc + jnp.where(inside, pltpu.roll(per_col, moved % cols, 1), 0.0)
        gathered_ref[row : row + 1] = acc
    gathered_ref[block_rows:] = jnp.zeros((gathered_ref.shape[0] - block_rows, cols), jnp.float32)
    span = pieces_ref.shape[2]
    width = span * FACTOR
    spread = (
        lax.broadcasted_iota(jnp.int32, (width, span), 0) // FACTOR
        == lax.broadcasted_iota(jnp.int32, (width, span), 1)
    ).astype(jnp.float32)
    for chunk in range(pieces_ref.shape[0]):
        pieces_ref[chunk] = jnp.dot(
            gathered_ref[:, chunk * width : (chunk + 1) * width], spread,
            precision=lax.Precision.HIGHEST, preferred_element_type=jnp.float32,
        )[:block_rows]


def march(drive, fwd, adj, src_above, src_below, dens, dens_above, dens_below, matched, block_rows, chunks):
    runs, waves, _, cols = src_above.shape
    rows = fwd.shape[1] + 2 * HALO
    vmem = pltpu.MemorySpace.VMEM
    smem = pltpu.MemorySpace.SMEM
    return pl.pallas_call(
        march_kernel,
        out_shape=(
            jax.ShapeDtypeStruct((waves, fwd.shape[1], cols), jnp.float32),
            jax.ShapeDtypeStruct((chunks, block_rows, 128), jnp.float32),
        ),
        in_specs=[pl.BlockSpec(memory_space=smem)] + [pl.BlockSpec(memory_space=vmem)] * 8,
        out_specs=(pl.BlockSpec(memory_space=vmem), pl.BlockSpec(memory_space=vmem)),
        scratch_shapes=[
            pltpu.VMEM((runs, waves, rows, cols), jnp.float32),
            pltpu.VMEM((rows, cols), jnp.float32),
            pltpu.VMEM((rows, cols), jnp.float32),
            pltpu.VMEM((ITERS, rows, cols), jnp.float32),
            pltpu.VMEM((rows, cols), jnp.float32),
            pltpu.VMEM((8, cols), jnp.float32),
        ],
    )(drive, fwd, adj, src_above, src_below, dens, dens_above, dens_below, matched)


def shards(density, foot_index, foot_weight, source_fwd, source_adj, omega):
    sources = jnp.stack([source_fwd, source_adj])
    src_above = from_behind(sources[:, :, -HALO:], "tile", 1)
    src_below = from_behind(sources[:, :, :HALO], "tile", -1)
    strip = gather_columns(density, "wl")
    block_rows, block_cols = strip.shape
    cells_x, cells_y = foot_index.shape[1:]
    factor = cells_y // block_cols
    assert factor == FACTOR and high_contrast / (source_fwd.shape[0] * lax.axis_size("wl")) == GRAD_SCALE
    weights = foot_weight.astype(jnp.float32)
    col_block = lax.broadcasted_iota(jnp.int32, (1, cells_y), 1) // factor
    key = (foot_index // block_cols) * len(SHIFTS) + (foot_index % block_cols - col_block[None]) + 2
    codes = lax.broadcasted_iota(jnp.int32, (block_rows * len(SHIFTS), 1, 1), 0)
    matched = jnp.zeros((block_rows * len(SHIFTS), cells_x, cells_y), jnp.float32)
    for entry in range(foot_index.shape[0]):
        matched = matched + jnp.where(key[entry][None] == codes, weights[entry][None], 0.0)
    matched = lax.optimization_barrier(matched)
    span = 128
    chunks = block_cols // span
    spread = (
        lax.broadcasted_iota(jnp.int32, (span, span * factor), 1) // factor
        == lax.broadcasted_iota(jnp.int32, (span, span * factor), 0)
    ).astype(jnp.float32)
    shifted = jnp.stack([lane_shift(strip[row], -shift) for row in range(block_rows) for shift in SHIFTS])
    candidates = jnp.dot(
        shifted.reshape(-1, span), spread, precision=lax.Precision.HIGHEST
    ).reshape(block_rows * len(SHIFTS), cells_y)
    reach = 2
    last_rows = jnp.sum(matched[:, -reach:] * candidates[:, None, :], axis=0)
    first_rows = jnp.sum(matched[:, :reach] * candidates[:, None, :], axis=0)
    present = jnp.ones((1, cells_y), jnp.float32)
    above = from_behind(jnp.concatenate([last_rows, present]), "tile", 1)
    below = from_behind(jnp.concatenate([present, first_rows]), "tile", -1)
    density_cell = jnp.sum(matched * candidates[:, None, :], axis=0)
    final, pieces = march(
        omega, source_fwd, source_adj, src_above, src_below, density_cell, above, below, matched, block_rows, chunks
    )
    count = lax.axis_size("wl")
    density_grad = lax.all_to_all(
        pieces.reshape(count, chunks // count, block_rows, span).transpose(0, 2, 1, 3).reshape(count, block_rows, -1),
        "wl", 0, 0, tiled=True,
    ).sum(axis=0)
    return (final, density_grad)


def solution(mesh):
    in_specs = (
        P("tile", "wl"),
        P(None, "tile", None),
        P(None, "tile", None),
        P("wl", "tile", None),
        P("wl", "tile", None),
        P("wl"),
    )
    out_specs = (P("wl", "tile", None), P("tile", "wl"))
    return jax.shard_map(shards, mesh=mesh, in_specs=in_specs, out_specs=out_specs, check_vma=False)
```

```python
import jax
import jax.numpy as jnp
from jax import lax
from jax.experimental import pallas as pl
from jax.experimental.pallas import tpu as pltpu
from jax.sharding import PartitionSpec as P

ITERS = 4
HALO = 4
FACTOR = 4
GRAD_SCALE = 4.0 / 16
SHIFTS = (-2, -1, 0, 1, 2)


time_step = 0.5
high_contrast = 4.0
drude_decay = 0.9
drude_gain = 0.5


def from_behind(value, axis, steps):
    count = lax.axis_size(axis)
    first, last = (max(0, -steps), min(count, count - steps))
    return lax.ppermute(value, axis, [(source, source + steps) for source in range(first, last)])


def with_halo(value, axis):
    above = from_behind(value[..., -HALO:, :], axis, 1)
    below = from_behind(value[..., :HALO, :], axis, -1)
    return jnp.concatenate([above, value, below], axis=-2)


def gather_columns(value, axis):
    count = lax.axis_size(axis)
    copies = jnp.broadcast_to(value[None], (count,) + value.shape)
    pieces = lax.all_to_all(copies, axis, 0, 0, tiled=True)
    return pieces.transpose(1, 0, 2).reshape(value.shape[0], count * value.shape[1])


def scatter_sum_columns(value, axis):
    count = lax.axis_size(axis)
    rows, cols = value.shape
    pieces = value.reshape(rows, count, cols // count).transpose(1, 0, 2)
    return lax.all_to_all(pieces, axis, 0, 0, tiled=True).sum(axis=0)


def lane_shift(vector, shift):
    width = vector.shape[-1]
    pad = [(0, 0)] * (vector.ndim - 1) + [(abs(shift), abs(shift))]
    padded = jnp.pad(vector, pad)
    start = abs(shift) - shift
    return lax.slice_in_dim(padded, start, start + width, axis=vector.ndim - 1)


def shifted_in(value, axis, shift):
    config = [(0, 0, 0)] * value.ndim
    size = value.shape[axis]
    if shift > 0:
        config[axis] = (shift, 0, 0)
        kept = lax.slice_in_dim(value, 0, size - shift, axis=axis)
    else:
        config[axis] = (0, -shift, 0)
        kept = lax.slice_in_dim(value, -shift, size, axis=axis)
    return lax.pad(kept, jnp.zeros((), value.dtype), config)


def march_kernel(
    drive_ref, fwd_ref, adj_ref, src_above_ref, src_below_ref,
    dens_ref, dens_above_ref, dens_below_ref, matched_ref,
    final_ref, pieces_ref,
    source_ref, density_ref, step_ref, history_ref, sense_ref, gathered_ref,
):
    runs, waves, rows, cols = source_ref.shape
    own = fwd_ref.shape[1]
    reach = dens_above_ref.shape[0] - 1
    block_rows = pieces_ref.shape[1]
    for wave in range(waves):
        for run, own_ref in enumerate((fwd_ref, adj_ref)):
            reach_src = src_above_ref.shape[2]
            source_ref[run, wave, 0 : HALO - reach_src] = jnp.zeros((HALO - reach_src, cols), jnp.float32)
            source_ref[run, wave, HALO - reach_src : HALO] = src_above_ref[run, wave]
            source_ref[run, wave, HALO : HALO + own] = own_ref[wave]
            source_ref[run, wave, HALO + own : HALO + own + reach_src] = src_below_ref[run, wave]
            source_ref[run, wave, HALO + own + reach_src : rows] = jnp.zeros((HALO - reach_src, cols), jnp.float32)
    density_ref[...] = jnp.zeros((rows, cols), jnp.float32)
    density_ref[HALO - reach : HALO] = dens_above_ref[0:reach]
    density_ref[HALO : HALO + own] = dens_ref[...]
    density_ref[HALO + own : HALO + own + reach] = dens_below_ref[1 : reach + 1]
    step_ref[0:HALO] = jnp.broadcast_to(time_step * dens_above_ref[reach : reach + 1], (HALO, cols))
    step_ref[HALO : HALO + own] = jnp.full((own, cols), time_step, jnp.float32)
    step_ref[HALO + own : rows] = jnp.broadcast_to(time_step * dens_below_ref[0:1], (HALO, cols))
    row_id = lax.broadcasted_iota(jnp.int32, (rows, cols), 0)
    col_id = lax.broadcasted_iota(jnp.int32, (rows, cols), 1)
    density = density_ref[...]
    half_density = drude_gain * density
    hy_step = step_ref[...]
    inverse = jnp.where(hy_step > 0.0, time_step / (1.0 + high_contrast * density), 0.0)
    sense_ref[...] = jnp.zeros((rows, cols), jnp.float32)
    drives = [
        [
            jnp.concatenate(
                [jnp.sin(jnp.full((rows, 128), drive_ref[wave] * (turn + 1.0), jnp.float32))] * (cols // 128), axis=1
            )
            for wave in range(waves)
        ]
        for turn in range(ITERS)
    ]
    for wave in range(waves):
        for run in range(runs):
            field_e = field_hx = field_hy = current = None
            for turn in range(ITERS):
                drive_term = drives[turn][wave] * source_ref[run, wave]
                if field_e is None:
                    field_e = drive_term
                else:
                    e_up = jnp.where(row_id < rows - 1, pltpu.roll(field_e, rows - 1, 0), 0.0)
                    e_right = jnp.where(col_id < cols - 1, pltpu.roll(field_e, cols - 1, 1), 0.0)
                    if field_hx is None:
                        field_hx = -time_step * (e_right - field_e)
                        field_hy = hy_step * (e_up - field_e)
                        current = half_density * field_e
                    else:
                        field_hx = field_hx - time_step * (e_right - field_e)
                        field_hy = field_hy + hy_step * (e_up - field_e)
                        current = drude_decay * current + half_density * field_e
                    hy_down = jnp.where(row_id > 0, pltpu.roll(field_hy, 1, 0), 0.0)
                    hx_left = jnp.where(col_id > 0, pltpu.roll(field_hx, 1, 1), 0.0)
                    field_e = (
                        field_e
                        + inverse * (field_hy - hy_down - (field_hx - hx_left) - current)
                        + drive_term
                    )
                if run == 0:
                    history_ref[turn] = field_e
                else:
                    sense_ref[...] += field_e * history_ref[ITERS - 1 - turn]
            if run == 0:
                final_ref[wave] = history_ref[ITERS - 1, HALO : HALO + own]
    scaled = GRAD_SCALE * sense_ref[HALO : HALO + own]
    lane = lax.broadcasted_iota(jnp.int32, (1, cols), 1)
    for row in range(block_rows):
        acc = jnp.zeros((1, cols), jnp.float32)
        for slot, shift in enumerate(SHIFTS):
            code = row * len(SHIFTS) + slot
            per_col = jnp.sum(matched_ref[code] * scaled, axis=0, keepdims=True)
            moved = FACTOR * shift
            inside = (lane >= moved) & (lane < cols + moved)
            acc = acc + jnp.where(inside, pltpu.roll(per_col, moved % cols, 1), 0.0)
        gathered_ref[row : row + 1] = acc
    gathered_ref[block_rows:] = jnp.zeros((gathered_ref.shape[0] - block_rows, cols), jnp.float32)
    span = pieces_ref.shape[2]
    width = span * FACTOR
    spread = (
        lax.broadcasted_iota(jnp.int32, (width, span), 0) // FACTOR
        == lax.broadcasted_iota(jnp.int32, (width, span), 1)
    ).astype(jnp.float32)
    for chunk in range(pieces_ref.shape[0]):
        pieces_ref[chunk] = jnp.dot(
            gathered_ref[:, chunk * width : (chunk + 1) * width], spread,
            precision=lax.Precision.HIGHEST, preferred_element_type=jnp.float32,
        )[:block_rows]


def march(drive, fwd, adj, src_above, src_below, dens, dens_above, dens_below, matched, block_rows, chunks):
    runs, waves, _, cols = src_above.shape
    rows = fwd.shape[1] + 2 * HALO
    vmem = pltpu.MemorySpace.VMEM
    smem = pltpu.MemorySpace.SMEM
    return pl.pallas_call(
        march_kernel,
        out_shape=(
            jax.ShapeDtypeStruct((waves, fwd.shape[1], cols), jnp.float32),
            jax.ShapeDtypeStruct((chunks, block_rows, 128), jnp.float32),
        ),
        in_specs=[pl.BlockSpec(memory_space=smem)] + [pl.BlockSpec(memory_space=vmem)] * 8,
        out_specs=(pl.BlockSpec(memory_space=vmem), pl.BlockSpec(memory_space=vmem)),
        scratch_shapes=[
            pltpu.VMEM((runs, waves, rows, cols), jnp.float32),
            pltpu.VMEM((rows, cols), jnp.float32),
            pltpu.VMEM((rows, cols), jnp.float32),
            pltpu.VMEM((ITERS, rows, cols), jnp.float32),
            pltpu.VMEM((rows, cols), jnp.float32),
            pltpu.VMEM((8, cols), jnp.float32),
        ],
    )(drive, fwd, adj, src_above, src_below, dens, dens_above, dens_below, matched)


def shards(density, foot_index, foot_weight, source_fwd, source_adj, omega):
    sources = jnp.stack([source_fwd, source_adj])
    src_above = from_behind(sources[:, :, -(ITERS - 1):], "tile", 1)
    src_below = from_behind(sources[:, :, : ITERS - 1], "tile", -1)
    strip = gather_columns(density, "wl")
    block_rows, block_cols = strip.shape
    cells_x, cells_y = foot_index.shape[1:]
    factor = cells_y // block_cols
    assert factor == FACTOR and high_contrast / (source_fwd.shape[0] * lax.axis_size("wl")) == GRAD_SCALE
    weights = foot_weight.astype(jnp.float32)
    col_block = lax.broadcasted_iota(jnp.int32, (1, cells_y), 1) // factor
    key = (foot_index // block_cols) * len(SHIFTS) + (foot_index % block_cols - col_block[None]) + 2
    codes = lax.broadcasted_iota(jnp.int32, (block_rows * len(SHIFTS), 1, 1), 0)
    matched = jnp.zeros((block_rows * len(SHIFTS), cells_x, cells_y), jnp.float32)
    for entry in range(foot_index.shape[0]):
        matched = matched + jnp.where(key[entry][None] == codes, weights[entry][None], 0.0)
    span = 128
    chunks = block_cols // span
    spread = (
        lax.broadcasted_iota(jnp.int32, (span, span * factor), 1) // factor
        == lax.broadcasted_iota(jnp.int32, (span, span * factor), 0)
    ).astype(jnp.float32)
    shifted = jnp.stack([lane_shift(strip[row], -shift) for row in range(block_rows) for shift in SHIFTS])
    candidates = jnp.dot(
        shifted.reshape(-1, span), spread, precision=lax.Precision.HIGHEST
    ).reshape(block_rows * len(SHIFTS), cells_y)
    reach = 2
    last_rows = jnp.sum(matched[:, -reach:] * candidates[:, None, :], axis=0)
    first_rows = jnp.sum(matched[:, :reach] * candidates[:, None, :], axis=0)
    present = jnp.ones((1, cells_y), jnp.float32)
    above = from_behind(jnp.concatenate([last_rows, present]), "tile", 1)
    below = from_behind(jnp.concatenate([present, first_rows]), "tile", -1)
    density_cell = jnp.sum(matched * candidates[:, None, :], axis=0)
    final, pieces = march(
        omega, source_fwd, source_adj, src_above, src_below, density_cell, above, below, matched, block_rows, chunks
    )
    count = lax.axis_size("wl")
    density_grad = lax.all_to_all(
        pieces.reshape(count, chunks // count, block_rows, span).transpose(0, 2, 1, 3).reshape(count, block_rows, -1),
        "wl", 0, 0, tiled=True,
    ).sum(axis=0)
    return (final, density_grad)


def solution(mesh):
    in_specs = (
        P("tile", "wl"),
        P(None, "tile", None),
        P(None, "tile", None),
        P("wl", "tile", None),
        P("wl", "tile", None),
        P("wl"),
    )
    out_specs = (P("wl", "tile", None), P("tile", "wl"))
    return jax.shard_map(shards, mesh=mesh, in_specs=in_specs, out_specs=out_specs, check_vma=False)
```

```python
import jax
import jax.numpy as jnp
from jax import lax
from jax.experimental import pallas as pl
from jax.experimental.pallas import tpu as pltpu
from jax.sharding import PartitionSpec as P

ITERS = 4
HALO = 4
FACTOR = 4
GRAD_SCALE = 4.0 / 16
SHIFTS = (-2, -1, 0, 1, 2)


time_step = 0.5
high_contrast = 4.0
drude_decay = 0.9
drude_gain = 0.5


def from_behind(value, axis, steps):
    count = lax.axis_size(axis)
    first, last = (max(0, -steps), min(count, count - steps))
    return lax.ppermute(value, axis, [(source, source + steps) for source in range(first, last)])


def with_halo(value, axis):
    above = from_behind(value[..., -HALO:, :], axis, 1)
    below = from_behind(value[..., :HALO, :], axis, -1)
    return jnp.concatenate([above, value, below], axis=-2)


def gather_columns(value, axis):
    count = lax.axis_size(axis)
    copies = jnp.broadcast_to(value[None], (count,) + value.shape)
    pieces = lax.all_to_all(copies, axis, 0, 0, tiled=True)
    return pieces.transpose(1, 0, 2).reshape(value.shape[0], count * value.shape[1])


def scatter_sum_columns(value, axis):
    count = lax.axis_size(axis)
    rows, cols = value.shape
    pieces = value.reshape(rows, count, cols // count).transpose(1, 0, 2)
    return lax.all_to_all(pieces, axis, 0, 0, tiled=True).sum(axis=0)


def lane_shift(vector, shift):
    width = vector.shape[-1]
    pad = [(0, 0)] * (vector.ndim - 1) + [(abs(shift), abs(shift))]
    padded = jnp.pad(vector, pad)
    start = abs(shift) - shift
    return lax.slice_in_dim(padded, start, start + width, axis=vector.ndim - 1)


def shifted_in(value, axis, shift):
    config = [(0, 0, 0)] * value.ndim
    size = value.shape[axis]
    if shift > 0:
        config[axis] = (shift, 0, 0)
        kept = lax.slice_in_dim(value, 0, size - shift, axis=axis)
    else:
        config[axis] = (0, -shift, 0)
        kept = lax.slice_in_dim(value, -shift, size, axis=axis)
    return lax.pad(kept, jnp.zeros((), value.dtype), config)


def march_kernel(
    drive_ref, fwd_ref, adj_ref, src_above_ref, src_below_ref,
    dens_ref, dens_above_ref, dens_below_ref, matched_ref,
    final_ref, pieces_ref,
    source_ref, density_ref, step_ref, history_ref, sense_ref, gathered_ref,
):
    runs, waves, rows, cols = source_ref.shape
    own = fwd_ref.shape[1]
    reach = dens_above_ref.shape[0] - 1
    block_rows = pieces_ref.shape[1]
    for wave in range(waves):
        for run, own_ref in enumerate((fwd_ref, adj_ref)):
            source_ref[run, wave, 0:HALO] = src_above_ref[run, wave]
            source_ref[run, wave, HALO : HALO + own] = own_ref[wave]
            source_ref[run, wave, HALO + own : rows] = src_below_ref[run, wave]
    density_ref[...] = jnp.zeros((rows, cols), jnp.float32)
    density_ref[HALO - reach : HALO] = dens_above_ref[0:reach]
    density_ref[HALO : HALO + own] = dens_ref[...]
    density_ref[HALO + own : HALO + own + reach] = dens_below_ref[1 : reach + 1]
    step_ref[0:HALO] = jnp.broadcast_to(time_step * dens_above_ref[reach : reach + 1], (HALO, cols))
    step_ref[HALO : HALO + own] = jnp.full((own, cols), time_step, jnp.float32)
    step_ref[HALO + own : rows] = jnp.broadcast_to(time_step * dens_below_ref[0:1], (HALO, cols))
    row_id = lax.broadcasted_iota(jnp.int32, (rows, cols), 0)
    col_id = lax.broadcasted_iota(jnp.int32, (rows, cols), 1)
    density = density_ref[...]
    half_density = drude_gain * density
    hy_step = step_ref[...]
    inverse = jnp.where(hy_step > 0.0, time_step / (1.0 + high_contrast * density), 0.0)
    sense_ref[...] = jnp.zeros((rows, cols), jnp.float32)
    drives = [
        [
            jnp.concatenate(
                [jnp.sin(jnp.full((rows, 128), drive_ref[wave] * (turn + 1.0), jnp.float32))] * (cols // 128), axis=1
            )
            for wave in range(waves)
        ]
        for turn in range(ITERS)
    ]
    for wave in range(waves):
        for run in range(runs):
            field_e = field_hx = field_hy = current = None
            for turn in range(ITERS):
                drive_term = drives[turn][wave] * source_ref[run, wave]
                if field_e is None:
                    field_e = drive_term
                else:
                    e_up = pltpu.roll(field_e, rows - 1, 0)
                    e_right = jnp.where(col_id < cols - 1, pltpu.roll(field_e, cols - 1, 1), 0.0)
                    if field_hx is None:
                        field_hx = -time_step * (e_right - field_e)
                        field_hy = hy_step * (e_up - field_e)
                        current = half_density * field_e
                    else:
                        field_hx = field_hx - time_step * (e_right - field_e)
                        field_hy = field_hy + hy_step * (e_up - field_e)
                        current = drude_decay * current + half_density * field_e
                    hy_down = pltpu.roll(field_hy, 1, 0)
                    hx_left = jnp.where(col_id > 0, pltpu.roll(field_hx, 1, 1), 0.0)
                    field_e = (
                        field_e
                        + inverse * (field_hy - hy_down - (field_hx - hx_left) - current)
                        + drive_term
                    )
                if run == 0:
                    history_ref[turn] = field_e
                else:
                    sense_ref[...] += field_e * history_ref[ITERS - 1 - turn]
            if run == 0:
                final_ref[wave] = history_ref[ITERS - 1, HALO : HALO + own]
    scaled = GRAD_SCALE * sense_ref[HALO : HALO + own]
    lane = lax.broadcasted_iota(jnp.int32, (1, cols), 1)
    for row in range(block_rows):
        acc = jnp.zeros((1, cols), jnp.float32)
        for slot, shift in enumerate(SHIFTS):
            code = row * len(SHIFTS) + slot
            per_col = jnp.sum(matched_ref[code] * scaled, axis=0, keepdims=True)
            moved = FACTOR * shift
            inside = (lane >= moved) & (lane < cols + moved)
            acc = acc + jnp.where(inside, pltpu.roll(per_col, moved % cols, 1), 0.0)
        gathered_ref[row : row + 1] = acc
    gathered_ref[block_rows:] = jnp.zeros((gathered_ref.shape[0] - block_rows, cols), jnp.float32)
    span = pieces_ref.shape[2]
    width = span * FACTOR
    spread = (
        lax.broadcasted_iota(jnp.int32, (width, span), 0) // FACTOR
        == lax.broadcasted_iota(jnp.int32, (width, span), 1)
    ).astype(jnp.float32)
    for chunk in range(pieces_ref.shape[0]):
        pieces_ref[chunk] = jnp.dot(
            gathered_ref[:, chunk * width : (chunk + 1) * width], spread,
            precision=lax.Precision.HIGHEST, preferred_element_type=jnp.float32,
        )[:block_rows]


def march(drive, fwd, adj, src_above, src_below, dens, dens_above, dens_below, matched, block_rows, chunks):
    runs, waves, _, cols = src_above.shape
    rows = fwd.shape[1] + 2 * HALO
    vmem = pltpu.MemorySpace.VMEM
    smem = pltpu.MemorySpace.SMEM
    return pl.pallas_call(
        march_kernel,
        out_shape=(
            jax.ShapeDtypeStruct((waves, fwd.shape[1], cols), jnp.float32),
            jax.ShapeDtypeStruct((chunks, block_rows, 128), jnp.float32),
        ),
        in_specs=[pl.BlockSpec(memory_space=smem)] + [pl.BlockSpec(memory_space=vmem)] * 8,
        out_specs=(pl.BlockSpec(memory_space=vmem), pl.BlockSpec(memory_space=vmem)),
        scratch_shapes=[
            pltpu.VMEM((runs, waves, rows, cols), jnp.float32),
            pltpu.VMEM((rows, cols), jnp.float32),
            pltpu.VMEM((rows, cols), jnp.float32),
            pltpu.VMEM((ITERS, rows, cols), jnp.float32),
            pltpu.VMEM((rows, cols), jnp.float32),
            pltpu.VMEM((8, cols), jnp.float32),
        ],
    )(drive, fwd, adj, src_above, src_below, dens, dens_above, dens_below, matched)


def shards(density, foot_index, foot_weight, source_fwd, source_adj, omega):
    sources = jnp.stack([source_fwd, source_adj])
    src_above = from_behind(sources[:, :, -HALO:], "tile", 1)
    src_below = from_behind(sources[:, :, :HALO], "tile", -1)
    strip = gather_columns(density, "wl")
    block_rows, block_cols = strip.shape
    cells_x, cells_y = foot_index.shape[1:]
    factor = cells_y // block_cols
    assert factor == FACTOR and high_contrast / (source_fwd.shape[0] * lax.axis_size("wl")) == GRAD_SCALE
    weights = foot_weight.astype(jnp.float32)
    col_block = lax.broadcasted_iota(jnp.int32, (1, cells_y), 1) // factor
    key = (foot_index // block_cols) * len(SHIFTS) + (foot_index % block_cols - col_block[None]) + 2
    codes = lax.broadcasted_iota(jnp.int32, (block_rows * len(SHIFTS), 1, 1), 0)
    matched = jnp.zeros((block_rows * len(SHIFTS), cells_x, cells_y), jnp.float32)
    for entry in range(foot_index.shape[0]):
        matched = matched + jnp.where(key[entry][None] == codes, weights[entry][None], 0.0)
    span = 128
    chunks = block_cols // span
    spread = (
        lax.broadcasted_iota(jnp.int32, (span, span * factor), 1) // factor
        == lax.broadcasted_iota(jnp.int32, (span, span * factor), 0)
    ).astype(jnp.float32)
    shifted = jnp.stack([lane_shift(strip[row], -shift) for row in range(block_rows) for shift in SHIFTS])
    candidates = jnp.dot(
        shifted.reshape(-1, span), spread, precision=lax.Precision.HIGHEST
    ).reshape(block_rows * len(SHIFTS), cells_y)
    reach = 2
    last_rows = jnp.sum(matched[:, -reach:] * candidates[:, None, :], axis=0)
    first_rows = jnp.sum(matched[:, :reach] * candidates[:, None, :], axis=0)
    present = jnp.ones((1, cells_y), jnp.float32)
    above = from_behind(jnp.concatenate([last_rows, present]), "tile", 1)
    below = from_behind(jnp.concatenate([present, first_rows]), "tile", -1)
    density_cell = jnp.sum(matched * candidates[:, None, :], axis=0)
    final, pieces = march(
        omega, source_fwd, source_adj, src_above, src_below, density_cell, above, below, matched, block_rows, chunks
    )
    count = lax.axis_size("wl")
    density_grad = lax.all_to_all(
        pieces.reshape(count, chunks // count, block_rows, span).transpose(0, 2, 1, 3).reshape(count, block_rows, -1),
        "wl", 0, 0, tiled=True,
    ).sum(axis=0)
    return (final, density_grad)


def solution(mesh):
    in_specs = (
        P("tile", "wl"),
        P(None, "tile", None),
        P(None, "tile", None),
        P("wl", "tile", None),
        P("wl", "tile", None),
        P("wl"),
    )
    out_specs = (P("wl", "tile", None), P("tile", "wl"))
    return jax.shard_map(shards, mesh=mesh, in_specs=in_specs, out_specs=out_specs, check_vma=False)
```
